32 devices in a mesh: rep: 4 (over y, core), exp: 8 (over z, x).
Axes of the slice: x: 2, y: 2, z: 4, core: 2. Of those that a mesh axis runs over, the one named last changes fastest.
Arguments:
- tokens: bfloat16 [8192, 1024], P(('rep', 'exp')), may hold values from -6 to 6
- cotangent: bfloat16 [8192, 1024], P(('rep', 'exp')), may hold values from -6 to 6
- expert_ids: int32 [8192, 8], P(('rep', 'exp')), may hold values from 0 to 15, as said below
- combine: bfloat16 [8192, 8], P(('rep', 'exp')), may hold values from 0.049804688 to 0.34960938
- gate_weight: bfloat16 [4, 16, 1024, 384], P('rep', 'exp'), may hold values from -0.1875 to 0.1875
- up_weight: bfloat16 [4, 16, 1024, 384], P('rep', 'exp'), may hold values from -0.1875 to 0.1875
- down_weight: bfloat16 [4, 16, 384, 1024], P('rep', 'exp'), may hold values from -0.625 to 0.625
- moment1: float32 [4, 16, 384, 1024], P('rep', 'exp'), may hold values from -4 to 4
- moment2: float32 [4, 16, 384, 1024], P('rep', 'exp'), may hold values from 0.01 to 1
- round_k: int32 [8], P('exp'), may hold values from 0 to 1
Outputs:
- mixed: bfloat16 [8192, 1024], P(('rep', 'exp'))
- input_grad: bfloat16 [8192, 1024], P(('rep', 'exp'))
- gate_grad: bfloat16 [4, 16, 1024, 384], P('rep', 'exp')
- up_grad: bfloat16 [4, 16, 1024, 384], P('rep', 'exp')
- new_down: bfloat16 [4, 16, 384, 1024], P('rep', 'exp')
- new_moment1: float32 [4, 16, 384, 1024], P('rep', 'exp')
- new_moment2: float32 [4, 16, 384, 1024], P('rep', 'exp')
The draws below stay inside these ranges and needn't reach their ends.
Inputs may be any that keep to these rules, and one draw needn't show every extreme that they name: `expert_ids`: each row names 8 different experts. Of the 256 rows of one device, at most 256 name any one expert, and at most 384 name one of the two experts 2i and 2i + 1; in every draw one expert is named by exactly 256 rows of every device, and one such pair of experts by exactly 384.
All inputs are finite; a program needn't handle non-finite values.
Results may differ from the reference program's by a relative error of at most 0.0064.
Values may be sent and summed in bfloat16 or wider, within the bound.
No kernel may reach another device: no remote copies, remote signals or barrier semaphores. Data moves between devices by JAX's collectives and lax.ppermute only.
A program may use at most 192 MiB of HBM per device.

```python
import math
from functools import partial
import jax
import jax.numpy as jnp
from jax import lax

D = 1024
HID = 384
TOPK = 8
EXP_DEV = 2
ROUNDS = 2
TOK_DEV = 256
REPLICAS = 4
EXPERTS = 16
TOKENS = 8192
CAP = 256
N_EXP = 8


def route_block(block_key, hottest):
    weight_key, order_key, row_key, turn_key = jax.random.split(block_key, 4)
    expert_iota = jnp.arange(EXPERTS, dtype=jnp.int32)
    partner = jnp.bitwise_xor(hottest, 1)
    is_other = (expert_iota != hottest) & (expert_iota != partner)
    weights = jax.random.randint(weight_key, (EXPERTS,), 7, 10).astype(jnp.int32)
    weights = jnp.where(is_other, weights, 0)
    spread_rows = TOK_DEV * TOPK - CAP - CAP // 2
    counts = weights * spread_rows // jnp.sum(weights)
    shortfall = spread_rows - jnp.sum(counts)
    expert_order = jax.random.permutation(order_key, EXPERTS).astype(jnp.int32)
    other_in_order = is_other[expert_order].astype(jnp.int32)
    rank_in_order = jnp.cumsum(other_in_order) - other_in_order
    ranking = jnp.zeros((EXPERTS,), jnp.int32).at[expert_order].set(rank_in_order.astype(jnp.int32))
    extra_one = ((ranking < shortfall) & is_other).astype(jnp.int32)
    counts = counts + extra_one
    counts = jnp.where(expert_iota == hottest, CAP, counts)
    counts = jnp.where(expert_iota == partner, CAP // 2, counts)
    run_ends = jnp.cumsum(counts)
    slot_iota = jnp.arange(TOK_DEV * TOPK, dtype=jnp.int32)
    slot_owner = jnp.sum((slot_iota[:, None] >= run_ends[None, :]).astype(jnp.int32), axis=1)
    row_table = slot_owner.reshape(TOPK, TOK_DEV).T
    row_table = row_table[jax.random.permutation(row_key, TOK_DEV)]
    row_turns = jax.random.randint(turn_key, (TOK_DEV, 1), 0, TOPK).astype(jnp.int32)
    column = (jnp.arange(TOPK, dtype=jnp.int32)[None, :] + row_turns) % TOPK
    return jnp.take_along_axis(row_table, column, axis=1)


def draw_expert_ids(key, part):
    hottest = jax.random.randint(jax.random.fold_in(key, 7), (), 0, EXPERTS).astype(jnp.int32)
    block_keys = jax.random.split(jax.random.fold_in(key, 11), TOKENS // TOK_DEV)
    blocks = jax.vmap(route_block, in_axes=(0, None))(block_keys, hottest)
    return blocks.reshape(TOKENS, TOPK).astype(jnp.int32)


def touch_ends(result, stream_key, low, high):
    index_at = [jax.random.randint(jax.random.fold_in(stream_key, axis), (), 0, length) for axis, length in enumerate(result.shape)]
    widest = result.shape.index(max(result.shape))
    beside = index_at[:widest] + [(index_at[widest] + 1) % result.shape[widest]] + index_at[widest + 1:]
    return result.at[tuple(index_at)].set(low).at[tuple(beside)].set(high)


def level_of(key, shape, shards, least, largest):
    def one(axis_at, shards_of):
        steps = jax.random.uniform(jax.random.fold_in(jax.random.fold_in(key, 6), axis_at), (shards_of,), jnp.float32, least / len(shards), largest / len(shards))
        return jnp.repeat(jnp.exp(steps), shape[axis_at] // shards_of).reshape((-1,) + (1,) * (len(shape) - axis_at - 1))

    loudness = one(*shards[0])
    for cut in shards[1:]:
        loudness = loudness * one(*cut)
    return loudness


def normal_values(rng, shape, deviation, bound, shards=(), kind=jnp.bfloat16):
    level = level_of(rng, shape, shards, -0.22, 0.18) if shards else 1.0
    values = jax.random.normal(rng, shape, jnp.float32) * deviation * level
    return jnp.minimum(jnp.maximum(values, -bound), bound).astype(kind)


def setup_inputs(seed: int = 0) -> dict:
    seeds = jax.random.split(jax.random.key(seed), 11)
    tokens = normal_values(seeds[0], (TOKENS, D), 1.0, 6.0, ((0, 32),))
    cotangent = normal_values(seeds[1], (TOKENS, D), 1.0, 6.0, ((0, 32),))
    expert_ids = draw_expert_ids(jax.random.fold_in(seeds[10], 71), 0)
    combine = jnp.clip(0.049804688 + 0.2998047 * jax.random.uniform(seeds[3], (TOKENS, TOPK), jnp.float32) ** level_of(seeds[3], (TOKENS, TOPK), ((0, 32),), -0.2, 0.2), 0.049804688, 0.34960938).astype(jnp.bfloat16)
    gate_weight = normal_values(seeds[4], (REPLICAS, EXPERTS, D, HID), D ** -0.5, 0.1875, ((0, 4), (1, 8)))
    up_weight = normal_values(seeds[5], (REPLICAS, EXPERTS, D, HID), D ** -0.5, 0.1875, ((0, 4), (1, 8)))
    down_weight = normal_values(seeds[6], (REPLICAS, EXPERTS, HID, D), (HID // 4) ** -0.5, 0.625, ((0, 4), (1, 8)))
    moment1 = normal_values(seeds[7], (REPLICAS, EXPERTS, HID, D), 0.5, 4.0, ((0, 4), (1, 8)), jnp.float32)
    moment2 = jnp.clip(jnp.exp(math.log(1.0) - 4.6051702 * jax.random.uniform(seeds[8], (REPLICAS, EXPERTS, HID, D), jnp.float32) ** level_of(seeds[8], (REPLICAS, EXPERTS, HID, D), ((0, 4), (1, 8)), -0.2, 0.2)), 0.01, 1.0)
    round_k = touch_ends(jax.random.randint(seeds[9], (N_EXP,), 0, ROUNDS), jax.random.fold_in(seeds[9], 1), 0, ROUNDS - 1).astype(jnp.int32)
    return dict(tokens=tokens, cotangent=cotangent, expert_ids=expert_ids, combine=combine, gate_weight=gate_weight, up_weight=up_weight, down_weight=down_weight, moment1=moment1, moment2=moment2, round_k=round_k)


beta_one = 0.9
beta_two = 0.999
learn_rate = 0.01
decay_rate = 0.1
adam_eps = 1e-08
step_count = 100.0

def slot_table(expert_ids, experts, capacity):
    flat_ids = expert_ids.reshape(-1).astype(jnp.int32)
    slot_total = flat_ids.shape[0]
    one_hot = (flat_ids[:, None] == jnp.arange(experts, dtype=jnp.int32)[None, :]).astype(jnp.int32)
    earlier = jnp.cumsum(one_hot, axis=0) - one_hot
    position = lax.optimization_barrier(jnp.sum(earlier * one_hot, axis=1))
    target = flat_ids * capacity + position
    filler = jnp.full((experts * capacity,), slot_total, jnp.int32)
    row_table = filler.at[target].set(jnp.arange(slot_total, dtype=jnp.int32))
    return (row_table.reshape(experts, capacity), target)

def expert_pass(expert_rows, cot_rows, weight_rows, gate_matrix, up_matrix, down_matrix):
    gate_value = jnp.dot(expert_rows, gate_matrix, preferred_element_type=jnp.float32)
    up_value = jnp.dot(expert_rows, up_matrix, preferred_element_type=jnp.float32)
    sigmoid_gate = jax.nn.sigmoid(gate_value)
    active = gate_value * sigmoid_gate
    hidden = (active * up_value).astype(jnp.bfloat16)
    expert_out = jnp.dot(hidden, down_matrix, preferred_element_type=jnp.float32).astype(jnp.bfloat16)
    slot_cot = (weight_rows.astype(jnp.float32)[:, None] * cot_rows.astype(jnp.float32)).astype(jnp.bfloat16)
    hidden_cot = jnp.dot(slot_cot, down_matrix.T, preferred_element_type=jnp.float32)
    gate_cot = (hidden_cot * up_value * sigmoid_gate * (1.0 + gate_value * (1.0 - sigmoid_gate))).astype(jnp.bfloat16)
    up_cot = (hidden_cot * active).astype(jnp.bfloat16)
    down_grad = jnp.dot(hidden.T, slot_cot, preferred_element_type=jnp.float32)
    gate_grad = jnp.dot(expert_rows.T, gate_cot, preferred_element_type=jnp.float32).astype(jnp.bfloat16)
    up_grad = jnp.dot(expert_rows.T, up_cot, preferred_element_type=jnp.float32).astype(jnp.bfloat16)
    input_cot = (jnp.dot(gate_cot, gate_matrix.T, preferred_element_type=jnp.float32) + jnp.dot(up_cot, up_matrix.T, preferred_element_type=jnp.float32)).astype(jnp.bfloat16)
    return (expert_out, input_cot, gate_grad, up_grad, down_grad)

def reference(tokens, cotangent, expert_ids, combine, gate_weight, up_weight, down_weight, moment1, moment2, round_k):
    group_rows = N_EXP * TOK_DEV
    slots_dev = TOK_DEV * TOPK
    expert_rounds = jnp.repeat(jnp.asarray(round_k).astype(jnp.int32), EXP_DEV)
    peer_down = down_weight
    for bit_index in range(ROUNDS):
        rolled = jnp.roll(down_weight, 1 << bit_index, axis=0)
        peer_down = jnp.where((expert_rounds == bit_index)[None, :, None, None], rolled, peer_down)
    bias_one = 1.0 - beta_one ** step_count
    bias_two = 1.0 - beta_two ** step_count
    mixed_parts, input_parts, gate_parts, up_parts = ([], [], [], [])
    down_parts, first_parts, second_parts = ([], [], [])
    for group_index in range(REPLICAS):
        row_start = group_index * group_rows
        group_tokens = tokens[row_start:row_start + group_rows]
        group_cot = cotangent[row_start:row_start + group_rows]
        group_ids = expert_ids[row_start:row_start + group_rows].reshape(N_EXP, TOK_DEV, TOPK)
        group_combine = combine[row_start:row_start + group_rows]
        tables, targets = jax.vmap(partial(slot_table, experts=EXPERTS, capacity=CAP))(group_ids)
        is_valid = tables < slots_dev
        device_iota = jnp.arange(N_EXP, dtype=jnp.int32)[:, None, None]
        row_index = jnp.where(is_valid, device_iota * TOK_DEV + tables // TOPK, group_rows)
        weight_index = jnp.where(is_valid, device_iota * slots_dev + tables, group_rows * TOPK)
        row_index = jnp.transpose(row_index, (1, 0, 2)).reshape(EXPERTS, N_EXP * CAP).astype(jnp.int32)
        weight_index = jnp.transpose(weight_index, (1, 0, 2)).reshape(EXPERTS, N_EXP * CAP).astype(jnp.int32)
        padded_tokens = jnp.concatenate([group_tokens, jnp.zeros((1, D), jnp.bfloat16)])
        padded_cot = jnp.concatenate([group_cot, jnp.zeros((1, D), jnp.bfloat16)])
        padded_weight = jnp.concatenate([group_combine.reshape(-1), jnp.zeros((1,), jnp.bfloat16)])

        def one_expert(packed):
            index_rows, index_weight, gate_matrix, up_matrix, down_matrix = packed
            return expert_pass(padded_tokens[index_rows], padded_cot[index_rows], padded_weight[index_weight], gate_matrix, up_matrix, down_matrix)
        expert_out, input_cot, gate_grad, up_grad, down_grad = lax.map(one_expert, (row_index, weight_index, gate_weight[group_index], up_weight[group_index], down_weight[group_index]))

        def to_slots(per_expert):
            by_device = jnp.transpose(per_expert.reshape(EXPERTS, N_EXP, CAP, D), (1, 0, 2, 3)).reshape(N_EXP, EXPERTS * CAP, D)
            picked = jax.vmap(lambda table_rows, index_rows: table_rows[index_rows])(by_device, targets)
            return picked.reshape(group_rows, TOPK, D).astype(jnp.float32)
        mixed_parts.append(lax.optimization_barrier(jnp.sum(group_combine.astype(jnp.float32)[:, :, None] * to_slots(expert_out), axis=1)).astype(jnp.bfloat16))
        input_parts.append(lax.optimization_barrier(jnp.sum(to_slots(input_cot), axis=1)).astype(jnp.bfloat16))
        gate_parts.append(gate_grad)
        up_parts.append(up_grad)
        first = beta_one * moment1[group_index] + (1.0 - beta_one) * down_grad
        second = beta_two * moment2[group_index] + (1.0 - beta_two) * down_grad * down_grad
        own_down = down_weight[group_index].astype(jnp.float32)
        averaged = (own_down + peer_down[group_index].astype(jnp.float32)) * 0.5
        update = first / bias_one / (jnp.sqrt(second / bias_two) + adam_eps)
        down_parts.append((averaged - learn_rate * (update + decay_rate * own_down)).astype(jnp.bfloat16))
        first_parts.append(first)
        second_parts.append(second)
    return (jnp.concatenate(mixed_parts), jnp.concatenate(input_parts), jnp.stack(gate_parts), jnp.stack(up_parts), jnp.stack(down_parts), jnp.stack(first_parts), jnp.stack(second_parts))
```

```python
import jax
import jax.numpy as jnp
from jax import lax
from jax.sharding import PartitionSpec as P

ROUNDS = 2
CHUNK_ROWS = 2048


beta_one = 0.9
beta_two = 0.999
learn_rate = 0.01
decay_rate = 0.1
adam_eps = 1e-08
step_count = 100.0


def shifted(value, axis, by):
    size = lax.axis_size(axis)
    return lax.ppermute(value, axis, [(i, (i + by) % size) for i in range(size)])


def dense_weights(expert_ids, combine, experts):
    expert_iota = jnp.arange(experts, dtype=jnp.int32)
    hit = expert_ids[:, :, None] == expert_iota[None, None, :]
    picked = jnp.where(hit, combine.astype(jnp.float32)[:, :, None], 0.0)
    return jnp.sum(picked, axis=1).astype(jnp.bfloat16)


def per_device(
    tokens,
    cotangent,
    expert_ids,
    combine,
    gate_weight,
    up_weight,
    down_weight,
    moment1,
    moment2,
    round_k,
):
    local_experts = gate_weight.shape[1]
    devices_exp = lax.axis_size("exp")
    experts = local_experts * devices_exp
    my_exp = lax.axis_index("exp")

    weight_table = dense_weights(expert_ids, combine, experts)
    group_weight = lax.all_gather(weight_table, "exp", axis=0, tiled=True)
    group_tokens = lax.all_gather(tokens, "exp", axis=0, tiled=True)
    group_cot = lax.all_gather(cotangent, "exp", axis=0, tiled=True)
    local_weight = lax.dynamic_slice_in_dim(
        group_weight, my_exp * local_experts, local_experts, axis=1
    ).astype(jnp.float32)
    local_weight = jnp.transpose(local_weight)[:, :, None]

    gate_matrix = gate_weight[0]
    up_matrix = up_weight[0]
    down_matrix = down_weight[0]

    def chunk_pass(chunk_tokens, chunk_cot, chunk_weight):
        gate_value = jnp.einsum(
            "td,edh->eth", chunk_tokens, gate_matrix, preferred_element_type=jnp.float32
        )
        up_value = jnp.einsum(
            "td,edh->eth", chunk_tokens, up_matrix, preferred_element_type=jnp.float32
        )
        sigmoid_gate = jax.nn.sigmoid(gate_value)
        active = gate_value * sigmoid_gate
        hidden = (active * up_value).astype(jnp.bfloat16)
        expert_out = jnp.einsum(
            "eth,ehd->etd", hidden, down_matrix, preferred_element_type=jnp.float32
        ).astype(jnp.bfloat16)
        mixed_part = jnp.sum(chunk_weight * expert_out.astype(jnp.float32), axis=0)
        slot_cot = (chunk_weight * chunk_cot.astype(jnp.float32)[None]).astype(jnp.bfloat16)
        hidden_cot = jnp.einsum(
            "etd,ehd->eth", slot_cot, down_matrix, preferred_element_type=jnp.float32
        )
        gate_cot = (
            hidden_cot * up_value * sigmoid_gate * (1.0 + gate_value * (1.0 - sigmoid_gate))
        ).astype(jnp.bfloat16)
        up_cot = (hidden_cot * active).astype(jnp.bfloat16)
        down_grad = jnp.einsum(
            "eth,etd->ehd", hidden, slot_cot, preferred_element_type=jnp.float32
        )
        gate_grad = jnp.einsum(
            "td,eth->edh", chunk_tokens, gate_cot, preferred_element_type=jnp.float32
        )
        up_grad = jnp.einsum(
            "td,eth->edh", chunk_tokens, up_cot, preferred_element_type=jnp.float32
        )
        input_cot = (
            jnp.einsum("eth,edh->etd", gate_cot, gate_matrix, preferred_element_type=jnp.float32)
            + jnp.einsum("eth,edh->etd", up_cot, up_matrix, preferred_element_type=jnp.float32)
        ).astype(jnp.bfloat16)
        input_part = jnp.sum(input_cot.astype(jnp.float32), axis=0)
        return mixed_part, input_part, gate_grad, up_grad, down_grad

    group_count = group_tokens.shape[0]
    chunk = min(group_count, CHUNK_ROWS)
    chunks = group_count // chunk
    if chunks == 1:
        mixed_part, input_part, gate_grad, up_grad, down_grad = chunk_pass(
            group_tokens, group_cot, local_weight
        )
    else:

        def step(carry, packed):
            parts = chunk_pass(*packed)
            grads = tuple(acc + part for acc, part in zip(carry, parts[2:]))
            return grads, parts[:2]

        zeros = (
            jnp.zeros(gate_matrix.shape, jnp.float32),
            jnp.zeros(up_matrix.shape, jnp.float32),
            jnp.zeros(down_matrix.shape, jnp.float32),
        )
        packed = (
            group_tokens.reshape(chunks, chunk, -1),
            group_cot.reshape(chunks, chunk, -1),
            jnp.transpose(local_weight.reshape(local_experts, chunks, chunk, 1), (1, 0, 2, 3)),
        )
        (gate_grad, up_grad, down_grad), (mixed_parts, input_parts) = lax.scan(
            step, zeros, packed
        )
        mixed_part = mixed_parts.reshape(group_count, -1)
        input_part = input_parts.reshape(group_count, -1)
    gate_grad = gate_grad.astype(jnp.bfloat16)
    up_grad = up_grad.astype(jnp.bfloat16)
    mixed = lax.psum_scatter(mixed_part, "exp", scatter_dimension=0, tiled=True).astype(
        jnp.bfloat16
    )
    input_grad = lax.psum_scatter(
        input_part, "exp", scatter_dimension=0, tiled=True
    ).astype(jnp.bfloat16)

    peers = [shifted(down_weight, "rep", 1 << bit_index) for bit_index in range(ROUNDS)]
    peer_down = peers[0]
    for bit_index in range(1, ROUNDS):
        peer_down = jnp.where(round_k[0] == bit_index, peers[bit_index], peer_down)
    bias_one = 1.0 - beta_one**step_count
    bias_two = 1.0 - beta_two**step_count
    first = beta_one * moment1[0] + (1.0 - beta_one) * down_grad
    second = beta_two * moment2[0] + (1.0 - beta_two) * down_grad * down_grad
    own_down = down_matrix.astype(jnp.float32)
    averaged = (own_down + peer_down[0].astype(jnp.float32)) * 0.5
    update = first / bias_one / (jnp.sqrt(second / bias_two) + adam_eps)
    new_down = (averaged - learn_rate * (update + decay_rate * own_down)).astype(jnp.bfloat16)
    return (
        mixed,
        input_grad,
        gate_grad[None],
        up_grad[None],
        new_down[None],
        first[None],
        second[None],
    )


def solution(mesh):
    return jax.shard_map(
        per_device,
        mesh=mesh,
        in_specs=(
            P(("rep", "exp"), None),
            P(("rep", "exp"), None),
            P(("rep", "exp"), None),
            P(("rep", "exp"), None),
            P("rep", "exp", None, None),
            P("rep", "exp", None, None),
            P("rep", "exp", None, None),
            P("rep", "exp", None, None),
            P("rep", "exp", None, None),
            P("exp"),
        ),
        out_specs=(
            P(("rep", "exp"), None),
            P(("rep", "exp"), None),
            P("rep", "exp", None, None),
            P("rep", "exp", None, None),
            P("rep", "exp", None, None),
            P("rep", "exp", None, None),
            P("rep", "exp", None, None),
        ),
        check_vma=False,
    )
```

```python
import jax
import jax.numpy as jnp
from jax import lax
from jax.sharding import PartitionSpec as P

ROUNDS = 2
CHUNK_ROWS = 2048


beta_one = 0.9
beta_two = 0.999
learn_rate = 0.01
decay_rate = 0.1
adam_eps = 1e-08
step_count = 100.0


def shifted(value, axis, by):
    size = lax.axis_size(axis)
    return lax.ppermute(value, axis, [(i, (i + by) % size) for i in range(size)])


def as_bf16(value):
    return lax.reduce_precision(value, exponent_bits=8, mantissa_bits=7)


def dense_weights(expert_ids, combine, experts):
    expert_iota = jnp.arange(experts, dtype=jnp.int32)
    hit = expert_ids[:, :, None] == expert_iota[None, None, :]
    picked = jnp.where(hit, combine.astype(jnp.float32)[:, :, None], 0.0)
    return jnp.sum(picked, axis=1).astype(jnp.bfloat16)


def per_device(
    tokens,
    cotangent,
    expert_ids,
    combine,
    gate_weight,
    up_weight,
    down_weight,
    moment1,
    moment2,
    round_k,
):
    local_experts = gate_weight.shape[1]
    devices_exp = lax.axis_size("exp")
    experts = local_experts * devices_exp
    my_exp = lax.axis_index("exp")

    token_count, model_width = tokens.shape
    weight_table = dense_weights(expert_ids, combine, experts)
    weight_rows = -(-(token_count * experts) // model_width)
    weight_rows = -(-weight_rows // 8) * 8
    weight_flat = jnp.pad(
        weight_table.reshape(-1), (0, weight_rows * model_width - token_count * experts)
    )
    packed_tokens = jnp.concatenate([tokens, weight_flat.reshape(weight_rows, model_width)])
    gathered = lax.all_gather(packed_tokens, "exp", axis=0, tiled=False)
    group_tokens = gathered[:, :token_count].reshape(devices_exp * token_count, model_width)
    group_weight = (
        gathered[:, token_count:]
        .reshape(devices_exp, -1)[:, : token_count * experts]
        .reshape(devices_exp * token_count, experts)
    )
    _, cotangent = lax.optimization_barrier((gathered, cotangent))
    group_cot = lax.all_gather(cotangent, "exp", axis=0, tiled=True)
    local_weight = lax.dynamic_slice_in_dim(
        group_weight, my_exp * local_experts, local_experts, axis=1
    ).astype(jnp.float32)
    local_weight = jnp.transpose(local_weight)[:, :, None]

    gate_matrix = gate_weight[0]
    up_matrix = up_weight[0]
    down_matrix = down_weight[0]

    def chunk_pass(chunk_tokens, chunk_cot, chunk_weight):
        gate_value = jnp.einsum(
            "td,edh->eth", chunk_tokens, gate_matrix, preferred_element_type=jnp.float32
        )
        up_value = jnp.einsum(
            "td,edh->eth", chunk_tokens, up_matrix, preferred_element_type=jnp.float32
        )
        sigmoid_gate = jax.nn.sigmoid(gate_value)
        active = gate_value * sigmoid_gate
        hidden = (active * up_value).astype(jnp.bfloat16)
        expert_out = as_bf16(
            jnp.einsum("eth,ehd->etd", hidden, down_matrix, preferred_element_type=jnp.float32)
        )
        mixed_part = jnp.sum(chunk_weight * expert_out, axis=0)
        slot_cot = (chunk_weight * chunk_cot.astype(jnp.float32)[None]).astype(jnp.bfloat16)
        hidden_cot = jnp.einsum(
            "etd,ehd->eth", slot_cot, down_matrix, preferred_element_type=jnp.float32
        )
        gate_cot = (
            hidden_cot * up_value * sigmoid_gate * (1.0 + gate_value * (1.0 - sigmoid_gate))
        ).astype(jnp.bfloat16)
        up_cot = (hidden_cot * active).astype(jnp.bfloat16)
        down_grad = jnp.einsum(
            "eth,etd->ehd", hidden, slot_cot, preferred_element_type=jnp.float32
        )
        gate_grad = jnp.einsum(
            "td,eth->edh", chunk_tokens, gate_cot, preferred_element_type=jnp.float32
        )
        up_grad = jnp.einsum(
            "td,eth->edh", chunk_tokens, up_cot, preferred_element_type=jnp.float32
        )
        input_cot = as_bf16(
            jnp.einsum("eth,edh->etd", gate_cot, gate_matrix, preferred_element_type=jnp.float32)
            + jnp.einsum("eth,edh->etd", up_cot, up_matrix, preferred_element_type=jnp.float32)
        )
        input_part = jnp.sum(input_cot, axis=0)
        return mixed_part, input_part, gate_grad, up_grad, down_grad

    group_count = group_tokens.shape[0]
    chunk = min(group_count, CHUNK_ROWS)
    chunks = group_count // chunk
    if chunks == 1:
        mixed_part, input_part, gate_grad, up_grad, down_grad = chunk_pass(
            group_tokens, group_cot, local_weight
        )
    else:

        def step(carry, packed):
            parts = chunk_pass(*packed)
            grads = tuple(acc + part for acc, part in zip(carry, parts[2:]))
            return grads, parts[:2]

        zeros = (
            jnp.zeros(gate_matrix.shape, jnp.float32),
            jnp.zeros(up_matrix.shape, jnp.float32),
            jnp.zeros(down_matrix.shape, jnp.float32),
        )
        packed = (
            group_tokens.reshape(chunks, chunk, -1),
            group_cot.reshape(chunks, chunk, -1),
            jnp.transpose(local_weight.reshape(local_experts, chunks, chunk, 1), (1, 0, 2, 3)),
        )
        (gate_grad, up_grad, down_grad), (mixed_parts, input_parts) = lax.scan(
            step, zeros, packed
        )
        mixed_part = mixed_parts.reshape(group_count, -1)
        input_part = input_parts.reshape(group_count, -1)
    gate_grad = gate_grad.astype(jnp.bfloat16)
    up_grad = up_grad.astype(jnp.bfloat16)
    mixed = lax.psum_scatter(mixed_part, "exp", scatter_dimension=0, tiled=True).astype(
        jnp.bfloat16
    )
    input_grad = lax.psum_scatter(
        input_part, "exp", scatter_dimension=0, tiled=True
    ).astype(jnp.bfloat16)

    peers = [shifted(down_weight, "rep", 1 << bit_index) for bit_index in range(ROUNDS)]
    peer_down = peers[0]
    for bit_index in range(1, ROUNDS):
        peer_down = jnp.where(round_k[0] == bit_index, peers[bit_index], peer_down)
    bias_one = 1.0 - beta_one**step_count
    bias_two = 1.0 - beta_two**step_count
    first = beta_one * moment1[0] + (1.0 - beta_one) * down_grad
    second = beta_two * moment2[0] + (1.0 - beta_two) * down_grad * down_grad
    own_down = down_matrix.astype(jnp.float32)
    averaged = (own_down + peer_down[0].astype(jnp.float32)) * 0.5
    update = first / bias_one / (jnp.sqrt(second / bias_two) + adam_eps)
    new_down = (averaged - learn_rate * (update + decay_rate * own_down)).astype(jnp.bfloat16)
    return (
        mixed,
        input_grad,
        gate_grad[None],
        up_grad[None],
        new_down[None],
        first[None],
        second[None],
    )


def solution(mesh):
    return jax.shard_map(
        per_device,
        mesh=mesh,
        in_specs=(
            P(("rep", "exp"), None),
            P(("rep", "exp"), None),
            P(("rep", "exp"), None),
            P(("rep", "exp"), None),
            P("rep", "exp", None, None),
            P("rep", "exp", None, None),
            P("rep", "exp", None, None),
            P("rep", "exp", None, None),
            P("rep", "exp", None, None),
            P("exp"),
        ),
        out_specs=(
            P(("rep", "exp"), None),
            P(("rep", "exp"), None),
            P("rep", "exp", None, None),
            P("rep", "exp", None, None),
            P("rep", "exp", None, None),
            P("rep", "exp", None, None),
            P("rep", "exp", None, None),
        ),
        check_vma=False,
    )
```

```python
import jax
import jax.numpy as jnp
from jax import lax
from jax.sharding import PartitionSpec as P

ROUNDS = 2
CHUNK_ROWS = 2048
RING_MAX = 8


beta_one = 0.9
beta_two = 0.999
learn_rate = 0.01
decay_rate = 0.1
adam_eps = 1e-08
step_count = 100.0


def shifted(value, axis, by):
    size = lax.axis_size(axis)
    return lax.ppermute(value, axis, [(i, (i + by) % size) for i in range(size)])


def as_bf16(value):
    return lax.reduce_precision(value, exponent_bits=8, mantissa_bits=7)


def dense_weights(expert_ids, combine, experts):
    expert_iota = jnp.arange(experts, dtype=jnp.int32)
    hit = expert_ids[:, :, None] == expert_iota[None, None, :]
    picked = jnp.where(hit, combine.astype(jnp.float32)[:, :, None], 0.0)
    return jnp.sum(picked, axis=1).astype(jnp.bfloat16)


def ring_order(size):
    return list(range(0, size, 2)) + list(range(size - 1 - size % 2, 0, -2))


def ring_pairs(ring, step):
    size = len(ring)
    return [(ring[q], ring[(q + step) % size]) for q in range(size)]


def ring_all_gather(shard, axis, ring):
    size = len(ring)
    ahead = size // 2
    behind = size - 1 - ahead
    got = {0: shard}
    current = shard
    for step in range(ahead):
        current = lax.ppermute(current, axis, ring_pairs(ring, 1))
        got[-(step + 1)] = current
    current = shard
    for step in range(behind):
        current = lax.ppermute(current, axis, ring_pairs(ring, -1))
        got[step + 1] = current
    return jnp.concatenate([got[offset] for offset in range(-ahead, behind + 1)])


def ring_reduce_scatter(part, axis, ring):
    size = len(ring)
    ahead = size // 2
    behind = size - 1 - ahead
    blocks = part.reshape((size, part.shape[0] // size) + part.shape[1:])

    def block_at(offset):
        return blocks[(offset + ahead) % size]

    result = block_at(0)
    if ahead:
        send = block_at(ahead)
        for step in range(ahead):
            received = lax.ppermute(send, axis, ring_pairs(ring, 1))
            if step < ahead - 1:
                send = received + block_at(ahead - step - 1)
        result = result + received
    if behind:
        send = block_at(-behind)
        for step in range(behind):
            received = lax.ppermute(send, axis, ring_pairs(ring, -1))
            if step < behind - 1:
                send = received + block_at(-behind + step + 1)
        result = result + received
    return result


def per_device(
    tokens,
    cotangent,
    expert_ids,
    combine,
    gate_weight,
    up_weight,
    down_weight,
    moment1,
    moment2,
    round_k,
):
    local_experts = gate_weight.shape[1]
    devices_exp = lax.axis_size("exp")
    experts = local_experts * devices_exp
    my_exp = lax.axis_index("exp")

    token_count, model_width = tokens.shape
    weight_table = dense_weights(expert_ids, combine, experts)
    weight_rows = -(-(token_count * experts) // model_width)
    weight_rows = -(-weight_rows // 8) * 8
    weight_flat = jnp.pad(
        weight_table.reshape(-1), (0, weight_rows * model_width - token_count * experts)
    )
    packed_tokens = jnp.concatenate([tokens, weight_flat.reshape(weight_rows, model_width)])
    ring = ring_order(devices_exp)
    use_ring = devices_exp <= RING_MAX

    def gather(value):
        if use_ring:
            return ring_all_gather(value, "exp", ring)
        return lax.all_gather(value, "exp", axis=0, tiled=True)

    def reduce_scatter(value):
        if use_ring:
            return ring_reduce_scatter(value, "exp", ring)
        return lax.psum_scatter(value, "exp", scatter_dimension=0, tiled=True)

    gathered = gather(packed_tokens[None])
    group_tokens = gathered[:, :token_count].reshape(devices_exp * token_count, model_width)
    group_weight = (
        gathered[:, token_count:]
        .reshape(devices_exp, -1)[:, : token_count * experts]
        .reshape(devices_exp * token_count, experts)
    )
    _, cotangent = lax.optimization_barrier((gathered, cotangent))
    group_cot = gather(cotangent)
    local_weight = lax.dynamic_slice_in_dim(
        group_weight, my_exp * local_experts, local_experts, axis=1
    ).astype(jnp.float32)
    local_weight = jnp.transpose(local_weight)[:, :, None]

    gate_matrix = gate_weight[0]
    up_matrix = up_weight[0]
    down_matrix = down_weight[0]

    def chunk_pass(chunk_tokens, chunk_cot, chunk_weight):
        gate_value = jnp.einsum(
            "td,edh->eth", chunk_tokens, gate_matrix, preferred_element_type=jnp.float32
        )
        up_value = jnp.einsum(
            "td,edh->eth", chunk_tokens, up_matrix, preferred_element_type=jnp.float32
        )
        sigmoid_gate = jax.nn.sigmoid(gate_value)
        active = gate_value * sigmoid_gate
        hidden = (active * up_value).astype(jnp.bfloat16)
        expert_out = as_bf16(
            jnp.einsum("eth,ehd->etd", hidden, down_matrix, preferred_element_type=jnp.float32)
        )
        mixed_part = jnp.sum(chunk_weight * expert_out, axis=0)
        slot_cot = (chunk_weight * chunk_cot.astype(jnp.float32)[None]).astype(jnp.bfloat16)
        hidden_cot = jnp.einsum(
            "etd,ehd->eth", slot_cot, down_matrix, preferred_element_type=jnp.float32
        )
        gate_cot = (
            hidden_cot * up_value * sigmoid_gate * (1.0 + gate_value * (1.0 - sigmoid_gate))
        ).astype(jnp.bfloat16)
        up_cot = (hidden_cot * active).astype(jnp.bfloat16)
        down_grad = jnp.einsum(
            "eth,etd->ehd", hidden, slot_cot, preferred_element_type=jnp.float32
        )
        gate_grad = jnp.einsum(
            "td,eth->edh", chunk_tokens, gate_cot, preferred_element_type=jnp.float32
        )
        up_grad = jnp.einsum(
            "td,eth->edh", chunk_tokens, up_cot, preferred_element_type=jnp.float32
        )
        input_cot = as_bf16(
            jnp.einsum("eth,edh->etd", gate_cot, gate_matrix, preferred_element_type=jnp.float32)
            + jnp.einsum("eth,edh->etd", up_cot, up_matrix, preferred_element_type=jnp.float32)
        )
        input_part = jnp.sum(input_cot, axis=0)
        return mixed_part, input_part, gate_grad, up_grad, down_grad

    group_count = group_tokens.shape[0]
    chunk = min(group_count, CHUNK_ROWS)
    chunks = group_count // chunk
    if chunks == 1:
        mixed_part, input_part, gate_grad, up_grad, down_grad = chunk_pass(
            group_tokens, group_cot, local_weight
        )
    else:

        def step(carry, packed):
            parts = chunk_pass(*packed)
            grads = tuple(acc + part for acc, part in zip(carry, parts[2:]))
            return grads, parts[:2]

        zeros = (
            jnp.zeros(gate_matrix.shape, jnp.float32),
            jnp.zeros(up_matrix.shape, jnp.float32),
            jnp.zeros(down_matrix.shape, jnp.float32),
        )
        packed = (
            group_tokens.reshape(chunks, chunk, -1),
            group_cot.reshape(chunks, chunk, -1),
            jnp.transpose(local_weight.reshape(local_experts, chunks, chunk, 1), (1, 0, 2, 3)),
        )
        (gate_grad, up_grad, down_grad), (mixed_parts, input_parts) = lax.scan(
            step, zeros, packed
        )
        mixed_part = mixed_parts.reshape(group_count, -1)
        input_part = input_parts.reshape(group_count, -1)
    gate_grad = gate_grad.astype(jnp.bfloat16)
    up_grad = up_grad.astype(jnp.bfloat16)
    mixed = reduce_scatter(mixed_part).astype(jnp.bfloat16)
    input_grad = reduce_scatter(input_part).astype(jnp.bfloat16)

    peers = [shifted(down_weight, "rep", 1 << bit_index) for bit_index in range(ROUNDS)]
    peer_down = peers[0]
    for bit_index in range(1, ROUNDS):
        peer_down = jnp.where(round_k[0] == bit_index, peers[bit_index], peer_down)
    bias_one = 1.0 - beta_one**step_count
    bias_two = 1.0 - beta_two**step_count
    first = beta_one * moment1[0] + (1.0 - beta_one) * down_grad
    second = beta_two * moment2[0] + (1.0 - beta_two) * down_grad * down_grad
    own_down = down_matrix.astype(jnp.float32)
    averaged = (own_down + peer_down[0].astype(jnp.float32)) * 0.5
    update = first / bias_one / (jnp.sqrt(second / bias_two) + adam_eps)
    new_down = (averaged - learn_rate * (update + decay_rate * own_down)).astype(jnp.bfloat16)
    return (
        mixed,
        input_grad,
        gate_grad[None],
        up_grad[None],
        new_down[None],
        first[None],
        second[None],
    )


def solution(mesh):
    return jax.shard_map(
        per_device,
        mesh=mesh,
        in_specs=(
            P(("rep", "exp"), None),
            P(("rep", "exp"), None),
            P(("rep", "exp"), None),
            P(("rep", "exp"), None),
            P("rep", "exp", None, None),
            P("rep", "exp", None, None),
            P("rep", "exp", None, None),
            P("rep", "exp", None, None),
            P("rep", "exp", None, None),
            P("exp"),
        ),
        out_specs=(
            P(("rep", "exp"), None),
            P(("rep", "exp"), None),
            P("rep", "exp", None, None),
            P("rep", "exp", None, None),
            P("rep", "exp", None, None),
            P("rep", "exp", None, None),
            P("rep", "exp", None, None),
        ),
        check_vma=False,
    )
```

```python
import jax
import jax.numpy as jnp
from jax import lax
from jax.sharding import PartitionSpec as P

ROUNDS = 2
CHUNK_ROWS = 2048
RING_MAX = 8


beta_one = 0.9
beta_two = 0.999
learn_rate = 0.01
decay_rate = 0.1
adam_eps = 1e-08
step_count = 100.0


def shifted(value, axis, by):
    size = lax.axis_size(axis)
    return lax.ppermute(value, axis, [(i, (i + by) % size) for i in range(size)])


def as_bf16(value):
    return lax.reduce_precision(value, exponent_bits=8, mantissa_bits=7)


def dense_weights(expert_ids, combine, experts):
    expert_iota = jnp.arange(experts, dtype=jnp.int32)
    hit = expert_ids[:, :, None] == expert_iota[None, None, :]
    picked = jnp.where(hit, combine.astype(jnp.float32)[:, :, None], 0.0)
    return jnp.sum(picked, axis=1).astype(jnp.bfloat16)


def ring_order(size):
    return list(range(0, size, 2)) + list(range(size - 1 - size % 2, 0, -2))


def ring_pairs(ring, step):
    size = len(ring)
    return [(ring[q], ring[(q + step) % size]) for q in range(size)]


def paired_shift(ahead_value, behind_value, axis, ring):
    if behind_value is None:
        return lax.ppermute(ahead_value, axis, ring_pairs(ring, 1)), None
    if ahead_value is None:
        return None, lax.ppermute(behind_value, axis, ring_pairs(ring, -1))
    ahead_value, behind_value = lax.optimization_barrier((ahead_value, behind_value))
    ahead_value = lax.ppermute(ahead_value, axis, ring_pairs(ring, 1))
    behind_value = lax.ppermute(behind_value, axis, ring_pairs(ring, -1))
    return lax.optimization_barrier((ahead_value, behind_value))


def ring_all_gather(shard, axis, ring):
    size = len(ring)
    ahead = size // 2
    behind = size - 1 - ahead
    got = {0: shard}
    ahead_value = shard
    behind_value = shard
    for step in range(max(ahead, behind)):
        ahead_value, behind_value = paired_shift(
            ahead_value if step < ahead else None,
            behind_value if step < behind else None,
            axis,
            ring,
        )
        if step < ahead:
            got[-(step + 1)] = ahead_value
        if step < behind:
            got[step + 1] = behind_value
    return jnp.concatenate([got[offset] for offset in range(-ahead, behind + 1)])


def ring_reduce_scatter(part, axis, ring):
    size = len(ring)
    ahead = size // 2
    behind = size - 1 - ahead
    blocks = part.reshape((size, part.shape[0] // size) + part.shape[1:])

    def block_at(offset):
        return blocks[(offset + ahead) % size]

    result = block_at(0)
    ahead_value = block_at(ahead) if ahead else None
    behind_value = block_at(-behind) if behind else None
    for step in range(max(ahead, behind)):
        ahead_value, behind_value = paired_shift(
            ahead_value if step < ahead else None,
            behind_value if step < behind else None,
            axis,
            ring,
        )
        if step < ahead - 1:
            ahead_value = ahead_value + block_at(ahead - step - 1)
        elif step == ahead - 1:
            result = result + ahead_value
        if step < behind - 1:
            behind_value = behind_value + block_at(-behind + step + 1)
        elif step == behind - 1:
            result = result + behind_value
    return result


def per_device(
    tokens,
    cotangent,
    expert_ids,
    combine,
    gate_weight,
    up_weight,
    down_weight,
    moment1,
    moment2,
    round_k,
):
    local_experts = gate_weight.shape[1]
    devices_exp = lax.axis_size("exp")
    experts = local_experts * devices_exp
    my_exp = lax.axis_index("exp")

    token_count, model_width = tokens.shape
    weight_table = dense_weights(expert_ids, combine, experts)
    weight_rows = -(-(token_count * experts) // model_width)
    weight_rows = -(-weight_rows // 8) * 8
    weight_flat = jnp.pad(
        weight_table.reshape(-1), (0, weight_rows * model_width - token_count * experts)
    )
    packed_tokens = jnp.concatenate([tokens, weight_flat.reshape(weight_rows, model_width)])
    ring = ring_order(devices_exp)
    use_ring = devices_exp <= RING_MAX

    def gather(value):
        if use_ring:
            return ring_all_gather(value, "exp", ring)
        return lax.all_gather(value, "exp", axis=0, tiled=True)

    def reduce_scatter(value):
        if use_ring:
            return ring_reduce_scatter(value, "exp", ring)
        return lax.psum_scatter(value, "exp", scatter_dimension=0, tiled=True)

    gathered = gather(packed_tokens[None])
    group_tokens = gathered[:, :token_count].reshape(devices_exp * token_count, model_width)
    group_weight = (
        gathered[:, token_count:]
        .reshape(devices_exp, -1)[:, : token_count * experts]
        .reshape(devices_exp * token_count, experts)
    )
    _, cotangent = lax.optimization_barrier((gathered, cotangent))
    group_cot = gather(cotangent)
    local_weight = lax.dynamic_slice_in_dim(
        group_weight, my_exp * local_experts, local_experts, axis=1
    ).astype(jnp.float32)
    local_weight = jnp.transpose(local_weight)[:, :, None]

    gate_matrix = gate_weight[0]
    up_matrix = up_weight[0]
    down_matrix = down_weight[0]

    def chunk_pass(chunk_tokens, chunk_cot, chunk_weight):
        gate_value = jnp.einsum(
            "td,edh->eth", chunk_tokens, gate_matrix, preferred_element_type=jnp.float32
        )
        up_value = jnp.einsum(
            "td,edh->eth", chunk_tokens, up_matrix, preferred_element_type=jnp.float32
        )
        sigmoid_gate = jax.nn.sigmoid(gate_value)
        active = gate_value * sigmoid_gate
        hidden = (active * up_value).astype(jnp.bfloat16)
        expert_out = as_bf16(
            jnp.einsum("eth,ehd->etd", hidden, down_matrix, preferred_element_type=jnp.float32)
        )
        mixed_part = jnp.sum(chunk_weight * expert_out, axis=0)
        slot_cot = (chunk_weight * chunk_cot.astype(jnp.float32)[None]).astype(jnp.bfloat16)
        hidden_cot = jnp.einsum(
            "etd,ehd->eth", slot_cot, down_matrix, preferred_element_type=jnp.float32
        )
        gate_cot = (
            hidden_cot * up_value * sigmoid_gate * (1.0 + gate_value * (1.0 - sigmoid_gate))
        ).astype(jnp.bfloat16)
        up_cot = (hidden_cot * active).astype(jnp.bfloat16)
        down_grad = jnp.einsum(
            "eth,etd->ehd", hidden, slot_cot, preferred_element_type=jnp.float32
        )
        gate_grad = jnp.einsum(
            "td,eth->edh", chunk_tokens, gate_cot, preferred_element_type=jnp.float32
        )
        up_grad = jnp.einsum(
            "td,eth->edh", chunk_tokens, up_cot, preferred_element_type=jnp.float32
        )
        input_cot = as_bf16(
            jnp.einsum("eth,edh->etd", gate_cot, gate_matrix, preferred_element_type=jnp.float32)
            + jnp.einsum("eth,edh->etd", up_cot, up_matrix, preferred_element_type=jnp.float32)
        )
        input_part = jnp.sum(input_cot, axis=0)
        return mixed_part, input_part, gate_grad, up_grad, down_grad

    group_count = group_tokens.shape[0]
    chunk = min(group_count, CHUNK_ROWS)
    chunks = group_count // chunk
    if chunks == 1:
        mixed_part, input_part, gate_grad, up_grad, down_grad = chunk_pass(
            group_tokens, group_cot, local_weight
        )
    else:

        def step(carry, packed):
            parts = chunk_pass(*packed)
            grads = tuple(acc + part for acc, part in zip(carry, parts[2:]))
            return grads, parts[:2]

        zeros = (
            jnp.zeros(gate_matrix.shape, jnp.float32),
            jnp.zeros(up_matrix.shape, jnp.float32),
            jnp.zeros(down_matrix.shape, jnp.float32),
        )
        packed = (
            group_tokens.reshape(chunks, chunk, -1),
            group_cot.reshape(chunks, chunk, -1),
            jnp.transpose(local_weight.reshape(local_experts, chunks, chunk, 1), (1, 0, 2, 3)),
        )
        (gate_grad, up_grad, down_grad), (mixed_parts, input_parts) = lax.scan(
            step, zeros, packed
        )
        mixed_part = mixed_parts.reshape(group_count, -1)
        input_part = input_parts.reshape(group_count, -1)
    gate_grad = gate_grad.astype(jnp.bfloat16)
    up_grad = up_grad.astype(jnp.bfloat16)
    mixed = reduce_scatter(mixed_part).astype(jnp.bfloat16)
    input_grad = reduce_scatter(input_part).astype(jnp.bfloat16)

    peers = [shifted(down_weight, "rep", 1 << bit_index) for bit_index in range(ROUNDS)]
    peer_down = peers[0]
    for bit_index in range(1, ROUNDS):
        peer_down = jnp.where(round_k[0] == bit_index, peers[bit_index], peer_down)
    bias_one = 1.0 - beta_one**step_count
    bias_two = 1.0 - beta_two**step_count
    first = beta_one * moment1[0] + (1.0 - beta_one) * down_grad
    second = beta_two * moment2[0] + (1.0 - beta_two) * down_grad * down_grad
    own_down = down_matrix.astype(jnp.float32)
    averaged = (own_down + peer_down[0].astype(jnp.float32)) * 0.5
    update = first / bias_one / (jnp.sqrt(second / bias_two) + adam_eps)
    new_down = (averaged - learn_rate * (update + decay_rate * own_down)).astype(jnp.bfloat16)
    return (
        mixed,
        input_grad,
        gate_grad[None],
        up_grad[None],
        new_down[None],
        first[None],
        second[None],
    )


def solution(mesh):
    return jax.shard_map(
        per_device,
        mesh=mesh,
        in_specs=(
            P(("rep", "exp"), None),
            P(("rep", "exp"), None),
            P(("rep", "exp"), None),
            P(("rep", "exp"), None),
            P("rep", "exp", None, None),
            P("rep", "exp", None, None),
            P("rep", "exp", None, None),
            P("rep", "exp", None, None),
            P("rep", "exp", None, None),
            P("exp"),
        ),
        out_specs=(
            P(("rep", "exp"), None),
            P(("rep", "exp"), None),
            P("rep", "exp", None, None),
            P("rep", "exp", None, None),
            P("rep", "exp", None, None),
            P("rep", "exp", None, None),
            P("rep", "exp", None, None),
        ),
        check_vma=False,
    )
```

```python
import jax
import jax.numpy as jnp
from jax import lax
from jax.sharding import PartitionSpec as P

ROUNDS = 2
CHUNK_ROWS = 2048
RING_MAX = 8


beta_one = 0.9
beta_two = 0.999
learn_rate = 0.01
decay_rate = 0.1
adam_eps = 1e-08
step_count = 100.0


def shifted(value, axis, by):
    size = lax.axis_size(axis)
    return lax.ppermute(value, axis, [(i, (i + by) % size) for i in range(size)])


def as_bf16(value):
    return lax.reduce_precision(value, exponent_bits=8, mantissa_bits=7)


def dense_weights(expert_ids, combine, experts):
    expert_iota = jnp.arange(experts, dtype=jnp.int32)
    hit = expert_ids[:, :, None] == expert_iota[None, None, :]
    picked = jnp.where(hit, combine.astype(jnp.float32)[:, :, None], 0.0)
    return jnp.sum(picked, axis=1).astype(jnp.bfloat16)


def ring_order(size):
    return list(range(0, size, 2)) + list(range(size - 1 - size % 2, 0, -2))


def ring_pairs(ring, step):
    size = len(ring)
    return [(ring[q], ring[(q + step) % size]) for q in range(size)]


def paired_shift(ahead_value, behind_value, axis, ring):
    if behind_value is None:
        return lax.ppermute(ahead_value, axis, ring_pairs(ring, 1)), None
    if ahead_value is None:
        return None, lax.ppermute(behind_value, axis, ring_pairs(ring, -1))
    ahead_value, behind_value = lax.optimization_barrier((ahead_value, behind_value))
    ahead_value = lax.ppermute(ahead_value, axis, ring_pairs(ring, 1))
    behind_value = lax.ppermute(behind_value, axis, ring_pairs(ring, -1))
    return lax.optimization_barrier((ahead_value, behind_value))


def ring_all_gather(shard, axis, ring):
    size = len(ring)
    ahead = size // 2
    behind = size - 1 - ahead
    got = {0: shard}
    ahead_value = shard
    behind_value = shard
    for step in range(max(ahead, behind)):
        ahead_value, behind_value = paired_shift(
            ahead_value if step < ahead else None,
            behind_value if step < behind else None,
            axis,
            ring,
        )
        if step < ahead:
            got[-(step + 1)] = ahead_value
        if step < behind:
            got[step + 1] = behind_value
    return jnp.concatenate([got[offset] for offset in range(-ahead, behind + 1)])


def ring_reduce_scatter(part, axis, ring, wire_dtype):
    size = len(ring)
    ahead = size // 2
    behind = size - 1 - ahead
    blocks = part.reshape((size, part.shape[0] // size) + part.shape[1:])

    def block_at(offset):
        return blocks[(offset + ahead) % size]

    def to_wire(value):
        return value.astype(wire_dtype)

    result = block_at(0)
    ahead_value = to_wire(block_at(ahead)) if ahead else None
    behind_value = to_wire(block_at(-behind)) if behind else None
    for step in range(max(ahead, behind)):
        ahead_value, behind_value = paired_shift(
            ahead_value if step < ahead else None,
            behind_value if step < behind else None,
            axis,
            ring,
        )
        if step < ahead - 1:
            ahead_value = to_wire(ahead_value.astype(part.dtype) + block_at(ahead - step - 1))
        elif step == ahead - 1:
            result = result + ahead_value.astype(part.dtype)
        if step < behind - 1:
            behind_value = to_wire(behind_value.astype(part.dtype) + block_at(-behind + step + 1))
        elif step == behind - 1:
            result = result + behind_value.astype(part.dtype)
    return result


def per_device(
    tokens,
    cotangent,
    expert_ids,
    combine,
    gate_weight,
    up_weight,
    down_weight,
    moment1,
    moment2,
    round_k,
):
    local_experts = gate_weight.shape[1]
    devices_exp = lax.axis_size("exp")
    experts = local_experts * devices_exp
    my_exp = lax.axis_index("exp")

    token_count, model_width = tokens.shape
    weight_table = dense_weights(expert_ids, combine, experts)
    weight_rows = -(-(token_count * experts) // model_width)
    weight_rows = -(-weight_rows // 8) * 8
    weight_flat = jnp.pad(
        weight_table.reshape(-1), (0, weight_rows * model_width - token_count * experts)
    )
    packed_tokens = jnp.concatenate([tokens, weight_flat.reshape(weight_rows, model_width)])
    ring = ring_order(devices_exp)
    use_ring = devices_exp <= RING_MAX

    def gather(value):
        if use_ring:
            return ring_all_gather(value, "exp", ring)
        return lax.all_gather(value, "exp", axis=0, tiled=True)

    def reduce_scatter(value):
        if use_ring:
            return ring_reduce_scatter(value, "exp", ring, jnp.bfloat16)
        return lax.psum_scatter(value, "exp", scatter_dimension=0, tiled=True)

    gathered = gather(packed_tokens[None])
    group_tokens = gathered[:, :token_count].reshape(devices_exp * token_count, model_width)
    group_weight = (
        gathered[:, token_count:]
        .reshape(devices_exp, -1)[:, : token_count * experts]
        .reshape(devices_exp * token_count, experts)
    )
    _, cotangent = lax.optimization_barrier((gathered, cotangent))
    group_cot = gather(cotangent)
    local_weight = lax.dynamic_slice_in_dim(
        group_weight, my_exp * local_experts, local_experts, axis=1
    ).astype(jnp.float32)
    local_weight = jnp.transpose(local_weight)[:, :, None]

    gate_matrix = gate_weight[0]
    up_matrix = up_weight[0]
    down_matrix = down_weight[0]

    def chunk_pass(chunk_tokens, chunk_cot, chunk_weight):
        gate_value = jnp.einsum(
            "td,edh->eth", chunk_tokens, gate_matrix, preferred_element_type=jnp.float32
        )
        up_value = jnp.einsum(
            "td,edh->eth", chunk_tokens, up_matrix, preferred_element_type=jnp.float32
        )
        sigmoid_gate = jax.nn.sigmoid(gate_value)
        active = gate_value * sigmoid_gate
        hidden = (active * up_value).astype(jnp.bfloat16)
        expert_out = as_bf16(
            jnp.einsum("eth,ehd->etd", hidden, down_matrix, preferred_element_type=jnp.float32)
        )
        mixed_part = jnp.sum(chunk_weight * expert_out, axis=0)
        slot_cot = (chunk_weight * chunk_cot.astype(jnp.float32)[None]).astype(jnp.bfloat16)
        hidden_cot = jnp.einsum(
            "etd,ehd->eth", slot_cot, down_matrix, preferred_element_type=jnp.float32
        )
        gate_cot = (
            hidden_cot * up_value * sigmoid_gate * (1.0 + gate_value * (1.0 - sigmoid_gate))
        ).astype(jnp.bfloat16)
        up_cot = (hidden_cot * active).astype(jnp.bfloat16)
        down_grad = jnp.einsum(
            "eth,etd->ehd", hidden, slot_cot, preferred_element_type=jnp.float32
        )
        gate_grad = jnp.einsum(
            "td,eth->edh", chunk_tokens, gate_cot, preferred_element_type=jnp.float32
        )
        up_grad = jnp.einsum(
            "td,eth->edh", chunk_tokens, up_cot, preferred_element_type=jnp.float32
        )
        input_cot = as_bf16(
            jnp.einsum("eth,edh->etd", gate_cot, gate_matrix, preferred_element_type=jnp.float32)
            + jnp.einsum("eth,edh->etd", up_cot, up_matrix, preferred_element_type=jnp.float32)
        )
        input_part = jnp.sum(input_cot, axis=0)
        return mixed_part, input_part, gate_grad, up_grad, down_grad

    group_count = group_tokens.shape[0]
    chunk = min(group_count, CHUNK_ROWS)
    chunks = group_count // chunk
    if chunks == 1:
        mixed_part, input_part, gate_grad, up_grad, down_grad = chunk_pass(
            group_tokens, group_cot, local_weight
        )
    else:

        def step(carry, packed):
            parts = chunk_pass(*packed)
            grads = tuple(acc + part for acc, part in zip(carry, parts[2:]))
            return grads, parts[:2]

        zeros = (
            jnp.zeros(gate_matrix.shape, jnp.float32),
            jnp.zeros(up_matrix.shape, jnp.float32),
            jnp.zeros(down_matrix.shape, jnp.float32),
        )
        packed = (
            group_tokens.reshape(chunks, chunk, -1),
            group_cot.reshape(chunks, chunk, -1),
            jnp.transpose(local_weight.reshape(local_experts, chunks, chunk, 1), (1, 0, 2, 3)),
        )
        (gate_grad, up_grad, down_grad), (mixed_parts, input_parts) = lax.scan(
            step, zeros, packed
        )
        mixed_part = mixed_parts.reshape(group_count, -1)
        input_part = input_parts.reshape(group_count, -1)
    gate_grad = gate_grad.astype(jnp.bfloat16)
    up_grad = up_grad.astype(jnp.bfloat16)
    mixed = reduce_scatter(mixed_part).astype(jnp.bfloat16)
    input_grad = reduce_scatter(input_part).astype(jnp.bfloat16)

    peers = [shifted(down_weight, "rep", 1 << bit_index) for bit_index in range(ROUNDS)]
    peer_down = peers[0]
    for bit_index in range(1, ROUNDS):
        peer_down = jnp.where(round_k[0] == bit_index, peers[bit_index], peer_down)
    bias_one = 1.0 - beta_one**step_count
    bias_two = 1.0 - beta_two**step_count
    first = beta_one * moment1[0] + (1.0 - beta_one) * down_grad
    second = beta_two * moment2[0] + (1.0 - beta_two) * down_grad * down_grad
    own_down = down_matrix.astype(jnp.float32)
    averaged = (own_down + peer_down[0].astype(jnp.float32)) * 0.5
    update = first / bias_one / (jnp.sqrt(second / bias_two) + adam_eps)
    new_down = (averaged - learn_rate * (update + decay_rate * own_down)).astype(jnp.bfloat16)
    return (
        mixed,
        input_grad,
        gate_grad[None],
        up_grad[None],
        new_down[None],
        first[None],
        second[None],
    )


def solution(mesh):
    return jax.shard_map(
        per_device,
        mesh=mesh,
        in_specs=(
            P(("rep", "exp"), None),
            P(("rep", "exp"), None),
            P(("rep", "exp"), None),
            P(("rep", "exp"), None),
            P("rep", "exp", None, None),
            P("rep", "exp", None, None),
            P("rep", "exp", None, None),
            P("rep", "exp", None, None),
            P("rep", "exp", None, None),
            P("exp"),
        ),
        out_specs=(
            P(("rep", "exp"), None),
            P(("rep", "exp"), None),
            P("rep", "exp", None, None),
            P("rep", "exp", None, None),
            P("rep", "exp", None, None),
            P("rep", "exp", None, None),
            P("rep", "exp", None, None),
        ),
        check_vma=False,
    )
```

```python
import jax
import jax.numpy as jnp
from jax import lax
from jax.sharding import PartitionSpec as P

ROUNDS = 2
CHUNK_ROWS = 2048
RING_MAX = 8


beta_one = 0.9
beta_two = 0.999
learn_rate = 0.01
decay_rate = 0.1
adam_eps = 1e-08
step_count = 100.0


def shifted(value, axis, by):
    size = lax.axis_size(axis)
    return lax.ppermute(value, axis, [(i, (i + by) % size) for i in range(size)])


def as_bf16(value):
    return lax.reduce_precision(value, exponent_bits=8, mantissa_bits=7)


def dense_weights(expert_ids, combine, experts):
    expert_iota = jnp.arange(experts, dtype=jnp.int32)
    hit = expert_ids[:, :, None] == expert_iota[None, None, :]
    picked = jnp.where(hit, combine.astype(jnp.float32)[:, :, None], 0.0)
    return jnp.sum(picked, axis=1).astype(jnp.bfloat16)


def ring_order(size):
    return list(range(0, size, 2)) + list(range(size - 1 - size % 2, 0, -2))


def ring_pairs(ring, step):
    size = len(ring)
    return [(ring[q], ring[(q + step) % size]) for q in range(size)]


def paired_shift(ahead_value, behind_value, axis, ring):
    if behind_value is None:
        return lax.ppermute(ahead_value, axis, ring_pairs(ring, 1)), None
    if ahead_value is None:
        return None, lax.ppermute(behind_value, axis, ring_pairs(ring, -1))
    ahead_value, behind_value = lax.optimization_barrier((ahead_value, behind_value))
    ahead_value = lax.ppermute(ahead_value, axis, ring_pairs(ring, 1))
    behind_value = lax.ppermute(behind_value, axis, ring_pairs(ring, -1))
    return lax.optimization_barrier((ahead_value, behind_value))


def ring_all_gather(shard, axis, ring):
    size = len(ring)
    ahead = size // 2
    behind = size - 1 - ahead
    got = {0: shard}
    ahead_value = shard
    behind_value = shard
    for step in range(max(ahead, behind)):
        ahead_value, behind_value = paired_shift(
            ahead_value if step < ahead else None,
            behind_value if step < behind else None,
            axis,
            ring,
        )
        if step < ahead:
            got[-(step + 1)] = ahead_value
        if step < behind:
            got[step + 1] = behind_value
    return jnp.concatenate([got[offset] for offset in range(-ahead, behind + 1)])


def ring_reduce_scatter(part, axis, ring, wire_dtype):
    size = len(ring)
    ahead = size // 2
    behind = size - 1 - ahead
    blocks = part.reshape((size, part.shape[0] // size) + part.shape[1:])

    def block_at(offset):
        return blocks[(offset + ahead) % size]

    def to_wire(value):
        return value.astype(wire_dtype)

    result = block_at(0)
    ahead_value = to_wire(block_at(ahead)) if ahead else None
    behind_value = to_wire(block_at(-behind)) if behind else None
    for step in range(max(ahead, behind)):
        ahead_value, behind_value = paired_shift(
            ahead_value if step < ahead else None,
            behind_value if step < behind else None,
            axis,
            ring,
        )
        if step < ahead - 1:
            ahead_value = to_wire(ahead_value.astype(part.dtype) + block_at(ahead - step - 1))
        elif step == ahead - 1:
            result = result + ahead_value.astype(part.dtype)
        if step < behind - 1:
            behind_value = to_wire(behind_value.astype(part.dtype) + block_at(-behind + step + 1))
        elif step == behind - 1:
            result = result + behind_value.astype(part.dtype)
    return result


def per_device(
    tokens,
    cotangent,
    expert_ids,
    combine,
    gate_weight,
    up_weight,
    down_weight,
    moment1,
    moment2,
    round_k,
):
    local_experts = gate_weight.shape[1]
    devices_exp = lax.axis_size("exp")
    experts = local_experts * devices_exp
    my_exp = lax.axis_index("exp")

    token_count, model_width = tokens.shape
    weight_table = dense_weights(expert_ids, combine, experts)
    weight_rows = -(-(token_count * experts) // model_width)
    weight_rows = -(-weight_rows // 8) * 8
    weight_flat = jnp.pad(
        weight_table.reshape(-1), (0, weight_rows * model_width - token_count * experts)
    )
    packed_tokens = jnp.concatenate([tokens, weight_flat.reshape(weight_rows, model_width)])
    ring = ring_order(devices_exp)
    use_ring = devices_exp <= RING_MAX

    def gather(value):
        if use_ring:
            return ring_all_gather(value, "exp", ring)
        return lax.all_gather(value, "exp", axis=0, tiled=True)

    def reduce_scatter(value):
        if use_ring:
            return ring_reduce_scatter(value, "exp", ring, jnp.bfloat16)
        return lax.psum_scatter(value, "exp", scatter_dimension=0, tiled=True)

    gathered = gather(packed_tokens[None])
    group_tokens = gathered[:, :token_count].reshape(devices_exp * token_count, model_width)
    group_weight = (
        gathered[:, token_count:]
        .reshape(devices_exp, -1)[:, : token_count * experts]
        .reshape(devices_exp * token_count, experts)
    )
    _, cotangent = lax.optimization_barrier((gathered, cotangent))
    group_cot = gather(cotangent)
    local_weight = lax.dynamic_slice_in_dim(
        group_weight, my_exp * local_experts, local_experts, axis=1
    ).astype(jnp.float32)
    local_weight = jnp.transpose(local_weight)[:, :, None]

    gate_matrix = gate_weight[0]
    up_matrix = up_weight[0]
    down_matrix = down_weight[0]

    def chunk_pass(chunk_tokens, chunk_cot, chunk_weight):
        gate_value = jnp.einsum(
            "td,edh->eth", chunk_tokens, gate_matrix, preferred_element_type=jnp.float32
        )
        up_value = jnp.einsum(
            "td,edh->eth", chunk_tokens, up_matrix, preferred_element_type=jnp.float32
        )
        sigmoid_gate = jax.nn.sigmoid(gate_value)
        active = gate_value * sigmoid_gate
        hidden = (active * up_value).astype(jnp.bfloat16)
        expert_out = as_bf16(
            jnp.einsum("eth,ehd->etd", hidden, down_matrix, preferred_element_type=jnp.float32)
        )
        mixed_part = jnp.sum(chunk_weight * expert_out, axis=0)
        chunk_cot, mixed_part = lax.optimization_barrier((chunk_cot, mixed_part))
        slot_cot = (chunk_weight * chunk_cot.astype(jnp.float32)[None]).astype(jnp.bfloat16)
        hidden_cot = jnp.einsum(
            "etd,ehd->eth", slot_cot, down_matrix, preferred_element_type=jnp.float32
        )
        gate_cot = (
            hidden_cot * up_value * sigmoid_gate * (1.0 + gate_value * (1.0 - sigmoid_gate))
        ).astype(jnp.bfloat16)
        up_cot = (hidden_cot * active).astype(jnp.bfloat16)
        down_grad = jnp.einsum(
            "eth,etd->ehd", hidden, slot_cot, preferred_element_type=jnp.float32
        )
        gate_grad = jnp.einsum(
            "td,eth->edh", chunk_tokens, gate_cot, preferred_element_type=jnp.float32
        )
        up_grad = jnp.einsum(
            "td,eth->edh", chunk_tokens, up_cot, preferred_element_type=jnp.float32
        )
        input_cot = as_bf16(
            jnp.einsum("eth,edh->etd", gate_cot, gate_matrix, preferred_element_type=jnp.float32)
            + jnp.einsum("eth,edh->etd", up_cot, up_matrix, preferred_element_type=jnp.float32)
        )
        input_part = jnp.sum(input_cot, axis=0)
        return mixed_part, input_part, gate_grad, up_grad, down_grad

    group_count = group_tokens.shape[0]
    chunk = min(group_count, CHUNK_ROWS)
    chunks = group_count // chunk
    if chunks == 1:
        mixed_part, input_part, gate_grad, up_grad, down_grad = chunk_pass(
            group_tokens, group_cot, local_weight
        )
    else:

        def step(carry, packed):
            parts = chunk_pass(*packed)
            grads = tuple(acc + part for acc, part in zip(carry, parts[2:]))
            return grads, parts[:2]

        zeros = (
            jnp.zeros(gate_matrix.shape, jnp.float32),
            jnp.zeros(up_matrix.shape, jnp.float32),
            jnp.zeros(down_matrix.shape, jnp.float32),
        )
        packed = (
            group_tokens.reshape(chunks, chunk, -1),
            group_cot.reshape(chunks, chunk, -1),
            jnp.transpose(local_weight.reshape(local_experts, chunks, chunk, 1), (1, 0, 2, 3)),
        )
        (gate_grad, up_grad, down_grad), (mixed_parts, input_parts) = lax.scan(
            step, zeros, packed
        )
        mixed_part = mixed_parts.reshape(group_count, -1)
        input_part = input_parts.reshape(group_count, -1)
    gate_grad = gate_grad.astype(jnp.bfloat16)
    up_grad = up_grad.astype(jnp.bfloat16)
    mixed = reduce_scatter(mixed_part).astype(jnp.bfloat16)
    input_grad = reduce_scatter(input_part).astype(jnp.bfloat16)

    peers = [shifted(down_weight, "rep", 1 << bit_index) for bit_index in range(ROUNDS)]
    peer_down = peers[0]
    for bit_index in range(1, ROUNDS):
        peer_down = jnp.where(round_k[0] == bit_index, peers[bit_index], peer_down)
    bias_one = 1.0 - beta_one**step_count
    bias_two = 1.0 - beta_two**step_count
    first = beta_one * moment1[0] + (1.0 - beta_one) * down_grad
    second = beta_two * moment2[0] + (1.0 - beta_two) * down_grad * down_grad
    own_down = down_matrix.astype(jnp.float32)
    averaged = (own_down + peer_down[0].astype(jnp.float32)) * 0.5
    update = first / bias_one / (jnp.sqrt(second / bias_two) + adam_eps)
    new_down = (averaged - learn_rate * (update + decay_rate * own_down)).astype(jnp.bfloat16)
    return (
        mixed,
        input_grad,
        gate_grad[None],
        up_grad[None],
        new_down[None],
        first[None],
        second[None],
    )


def solution(mesh):
    return jax.shard_map(
        per_device,
        mesh=mesh,
        in_specs=(
            P(("rep", "exp"), None),
            P(("rep", "exp"), None),
            P(("rep", "exp"), None),
            P(("rep", "exp"), None),
            P("rep", "exp", None, None),
            P("rep", "exp", None, None),
            P("rep", "exp", None, None),
            P("rep", "exp", None, None),
            P("rep", "exp", None, None),
            P("exp"),
        ),
        out_specs=(
            P(("rep", "exp"), None),
            P(("rep", "exp"), None),
            P("rep", "exp", None, None),
            P("rep", "exp", None, None),
            P("rep", "exp", None, None),
            P("rep", "exp", None, None),
            P("rep", "exp", None, None),
        ),
        check_vma=False,
    )
```

```python
import jax
import jax.numpy as jnp
from jax import lax
from jax.sharding import PartitionSpec as P

ROUNDS = 2
CHUNK_ROWS = 2048
RING_MAX = 8


beta_one = 0.9
beta_two = 0.999
learn_rate = 0.01
decay_rate = 0.1
adam_eps = 1e-08
step_count = 100.0


def shifted(value, axis, by):
    size = lax.axis_size(axis)
    return lax.ppermute(value, axis, [(i, (i + by) % size) for i in range(size)])


def as_bf16(value):
    return lax.reduce_precision(value, exponent_bits=8, mantissa_bits=7)


def dense_weights(expert_ids, combine, experts):
    expert_iota = jnp.arange(experts, dtype=jnp.int32)
    hit = expert_ids[:, :, None] == expert_iota[None, None, :]
    picked = jnp.where(hit, combine.astype(jnp.float32)[:, :, None], 0.0)
    return jnp.sum(picked, axis=1).astype(jnp.bfloat16)


def ring_order(size):
    return list(range(0, size, 2)) + list(range(size - 1 - size % 2, 0, -2))


def ring_pairs(ring, step):
    size = len(ring)
    return [(ring[q], ring[(q + step) % size]) for q in range(size)]


def paired_shift(ahead_value, behind_value, axis, ring):
    if behind_value is None:
        return lax.ppermute(ahead_value, axis, ring_pairs(ring, 1)), None
    if ahead_value is None:
        return None, lax.ppermute(behind_value, axis, ring_pairs(ring, -1))
    ahead_value, behind_value = lax.optimization_barrier((ahead_value, behind_value))
    ahead_value = lax.ppermute(ahead_value, axis, ring_pairs(ring, 1))
    behind_value = lax.ppermute(behind_value, axis, ring_pairs(ring, -1))
    return lax.optimization_barrier((ahead_value, behind_value))


def ring_all_gather(shard, axis, ring):
    size = len(ring)
    ahead = size // 2
    behind = size - 1 - ahead
    got = {0: shard}
    ahead_value = shard
    behind_value = shard
    for step in range(max(ahead, behind)):
        ahead_value, behind_value = paired_shift(
            ahead_value if step < ahead else None,
            behind_value if step < behind else None,
            axis,
            ring,
        )
        if step < ahead:
            got[-(step + 1)] = ahead_value
        if step < behind:
            got[step + 1] = behind_value
    return jnp.concatenate([got[offset] for offset in range(-ahead, behind + 1)])


def ring_reduce_scatter(part, axis, ring, wire_dtype):
    size = len(ring)
    ahead = size // 2
    behind = size - 1 - ahead
    blocks = part.reshape((size, part.shape[0] // size) + part.shape[1:])

    def block_at(offset):
        return blocks[(offset + ahead) % size]

    def to_wire(value):
        return value.astype(wire_dtype)

    result = block_at(0)
    ahead_value = to_wire(block_at(ahead)) if ahead else None
    behind_value = to_wire(block_at(-behind)) if behind else None
    for step in range(max(ahead, behind)):
        ahead_value, behind_value = paired_shift(
            ahead_value if step < ahead else None,
            behind_value if step < behind else None,
            axis,
            ring,
        )
        if step < ahead - 1:
            ahead_value = to_wire(ahead_value.astype(part.dtype) + block_at(ahead - step - 1))
        elif step == ahead - 1:
            result = result + ahead_value.astype(part.dtype)
        if step < behind - 1:
            behind_value = to_wire(behind_value.astype(part.dtype) + block_at(-behind + step + 1))
        elif step == behind - 1:
            result = result + behind_value.astype(part.dtype)
    return result


def per_device(
    tokens,
    cotangent,
    expert_ids,
    combine,
    gate_weight,
    up_weight,
    down_weight,
    moment1,
    moment2,
    round_k,
):
    local_experts = gate_weight.shape[1]
    devices_exp = lax.axis_size("exp")
    experts = local_experts * devices_exp
    my_exp = lax.axis_index("exp")

    token_count, model_width = tokens.shape
    weight_table = dense_weights(expert_ids, combine, experts)
    weight_rows = -(-(token_count * experts) // model_width)
    weight_rows = -(-weight_rows // 8) * 8
    weight_flat = jnp.pad(
        weight_table.reshape(-1), (0, weight_rows * model_width - token_count * experts)
    )
    packed_tokens = jnp.concatenate([tokens, weight_flat.reshape(weight_rows, model_width)])
    ring = ring_order(devices_exp)
    use_ring = devices_exp <= RING_MAX

    def gather(value):
        if use_ring:
            return ring_all_gather(value, "exp", ring)
        return lax.all_gather(value, "exp", axis=0, tiled=True)

    def reduce_scatter(value):
        if use_ring:
            return ring_reduce_scatter(value, "exp", ring, jnp.bfloat16)
        return lax.psum_scatter(value, "exp", scatter_dimension=0, tiled=True)

    gathered = gather(packed_tokens[None])
    group_tokens = gathered[:, :token_count].reshape(devices_exp * token_count, model_width)
    group_weight = (
        gathered[:, token_count:]
        .reshape(devices_exp, -1)[:, : token_count * experts]
        .reshape(devices_exp * token_count, experts)
    )
    _, cotangent = lax.optimization_barrier((gathered, cotangent))
    group_cot = gather(cotangent)
    local_weight = lax.dynamic_slice_in_dim(
        group_weight, my_exp * local_experts, local_experts, axis=1
    ).astype(jnp.float32)
    local_weight = jnp.transpose(local_weight)[:, :, None]

    gate_matrix = gate_weight[0]
    up_matrix = up_weight[0]
    down_matrix = down_weight[0]

    def chunk_pass(chunk_tokens, chunk_cot, chunk_weight):
        gate_value = jnp.einsum(
            "td,edh->eth", chunk_tokens, gate_matrix, preferred_element_type=jnp.float32
        )
        up_value = jnp.einsum(
            "td,edh->eth", chunk_tokens, up_matrix, preferred_element_type=jnp.float32
        )
        sigmoid_gate = jax.nn.sigmoid(gate_value)
        active = gate_value * sigmoid_gate
        hidden = (active * up_value).astype(jnp.bfloat16)
        expert_out = as_bf16(
            jnp.einsum("eth,ehd->etd", hidden, down_matrix, preferred_element_type=jnp.float32)
        )
        mixed_part = jnp.sum(chunk_weight * expert_out, axis=0)
        chunk_cot, mixed_part = lax.optimization_barrier((chunk_cot, mixed_part))
        slot_cot = (chunk_weight * chunk_cot.astype(jnp.float32)[None]).astype(jnp.bfloat16)
        hidden_cot = jnp.einsum(
            "etd,ehd->eth", slot_cot, down_matrix, preferred_element_type=jnp.float32
        )
        gate_cot = (
            hidden_cot * up_value * sigmoid_gate * (1.0 + gate_value * (1.0 - sigmoid_gate))
        ).astype(jnp.bfloat16)
        up_cot = (hidden_cot * active).astype(jnp.bfloat16)
        down_grad = jnp.einsum(
            "eth,etd->ehd", hidden, slot_cot, preferred_element_type=jnp.float32
        )
        gate_grad = jnp.einsum(
            "td,eth->edh", chunk_tokens, gate_cot, preferred_element_type=jnp.float32
        )
        up_grad = jnp.einsum(
            "td,eth->edh", chunk_tokens, up_cot, preferred_element_type=jnp.float32
        )
        input_cot = as_bf16(
            jnp.einsum("eth,edh->etd", gate_cot, gate_matrix, preferred_element_type=jnp.float32)
            + jnp.einsum("eth,edh->etd", up_cot, up_matrix, preferred_element_type=jnp.float32)
        )
        input_part = jnp.sum(input_cot, axis=0)
        return mixed_part, input_part, gate_grad, up_grad, down_grad

    group_count = group_tokens.shape[0]
    chunk = min(group_count, CHUNK_ROWS)
    chunks = group_count // chunk
    if chunks == 1:
        mixed_part, input_part, gate_grad, up_grad, down_grad = chunk_pass(
            group_tokens, group_cot, local_weight
        )
    else:

        def step(carry, packed):
            parts = chunk_pass(*packed)
            grads = tuple(acc + part for acc, part in zip(carry, parts[2:]))
            return grads, parts[:2]

        zeros = (
            jnp.zeros(gate_matrix.shape, jnp.float32),
            jnp.zeros(up_matrix.shape, jnp.float32),
            jnp.zeros(down_matrix.shape, jnp.float32),
        )
        packed = (
            group_tokens.reshape(chunks, chunk, -1),
            group_cot.reshape(chunks, chunk, -1),
            jnp.transpose(local_weight.reshape(local_experts, chunks, chunk, 1), (1, 0, 2, 3)),
        )
        (gate_grad, up_grad, down_grad), (mixed_parts, input_parts) = lax.scan(
            step, zeros, packed
        )
        mixed_part = mixed_parts.reshape(group_count, -1)
        input_part = input_parts.reshape(group_count, -1)
    gate_grad = gate_grad.astype(jnp.bfloat16)
    up_grad = up_grad.astype(jnp.bfloat16)
    mixed = reduce_scatter(mixed_part)
    input_part, mixed = lax.optimization_barrier((input_part, mixed))
    mixed = mixed.astype(jnp.bfloat16)
    input_grad = reduce_scatter(input_part).astype(jnp.bfloat16)

    peers = [shifted(down_weight, "rep", 1 << bit_index) for bit_index in range(ROUNDS)]
    peer_down = peers[0]
    for bit_index in range(1, ROUNDS):
        peer_down = jnp.where(round_k[0] == bit_index, peers[bit_index], peer_down)
    bias_one = 1.0 - beta_one**step_count
    bias_two = 1.0 - beta_two**step_count
    first = beta_one * moment1[0] + (1.0 - beta_one) * down_grad
    second = beta_two * moment2[0] + (1.0 - beta_two) * down_grad * down_grad
    own_down = down_matrix.astype(jnp.float32)
    averaged = (own_down + peer_down[0].astype(jnp.float32)) * 0.5
    update = first / bias_one / (jnp.sqrt(second / bias_two) + adam_eps)
    new_down = (averaged - learn_rate * (update + decay_rate * own_down)).astype(jnp.bfloat16)
    return (
        mixed,
        input_grad,
        gate_grad[None],
        up_grad[None],
        new_down[None],
        first[None],
        second[None],
    )


def solution(mesh):
    return jax.shard_map(
        per_device,
        mesh=mesh,
        in_specs=(
            P(("rep", "exp"), None),
            P(("rep", "exp"), None),
            P(("rep", "exp"), None),
            P(("rep", "exp"), None),
            P("rep", "exp", None, None),
            P("rep", "exp", None, None),
            P("rep", "exp", None, None),
            P("rep", "exp", None, None),
            P("rep", "exp", None, None),
            P("exp"),
        ),
        out_specs=(
            P(("rep", "exp"), None),
            P(("rep", "exp"), None),
            P("rep", "exp", None, None),
            P("rep", "exp", None, None),
            P("rep", "exp", None, None),
            P("rep", "exp", None, None),
            P("rep", "exp", None, None),
        ),
        check_vma=False,
    )
```

```python
import jax
import jax.numpy as jnp
from jax import lax
from jax.sharding import PartitionSpec as P

ROUNDS = 2
CHUNK_ROWS = 2048
RING_MAX = 8
SLICES = 2


beta_one = 0.9
beta_two = 0.999
learn_rate = 0.01
decay_rate = 0.1
adam_eps = 1e-08
step_count = 100.0


def shifted(value, axis, by):
    size = lax.axis_size(axis)
    return lax.ppermute(value, axis, [(i, (i + by) % size) for i in range(size)])


def as_bf16(value):
    return lax.reduce_precision(value, exponent_bits=8, mantissa_bits=7)


def dense_weights(expert_ids, combine, experts):
    expert_iota = jnp.arange(experts, dtype=jnp.int32)
    hit = expert_ids[:, :, None] == expert_iota[None, None, :]
    picked = jnp.where(hit, combine.astype(jnp.float32)[:, :, None], 0.0)
    return jnp.sum(picked, axis=1).astype(jnp.bfloat16)


def ring_order(size):
    return list(range(0, size, 2)) + list(range(size - 1 - size % 2, 0, -2))


def ring_pairs(ring, step):
    size = len(ring)
    return [(ring[q], ring[(q + step) % size]) for q in range(size)]


def paired_shift(ahead_value, behind_value, axis, ring):
    if behind_value is None:
        return lax.ppermute(ahead_value, axis, ring_pairs(ring, 1)), None
    if ahead_value is None:
        return None, lax.ppermute(behind_value, axis, ring_pairs(ring, -1))
    ahead_value, behind_value = lax.optimization_barrier((ahead_value, behind_value))
    ahead_value = lax.ppermute(ahead_value, axis, ring_pairs(ring, 1))
    behind_value = lax.ppermute(behind_value, axis, ring_pairs(ring, -1))
    return lax.optimization_barrier((ahead_value, behind_value))


def ring_all_gather(shard, axis, ring):
    size = len(ring)
    ahead = size // 2
    behind = size - 1 - ahead
    got = {0: shard}
    ahead_value = shard
    behind_value = shard
    for step in range(max(ahead, behind)):
        ahead_value, behind_value = paired_shift(
            ahead_value if step < ahead else None,
            behind_value if step < behind else None,
            axis,
            ring,
        )
        if step < ahead:
            got[-(step + 1)] = ahead_value
        if step < behind:
            got[step + 1] = behind_value
    return jnp.concatenate([got[offset] for offset in range(-ahead, behind + 1)])


def ring_reduce_scatter(part, axis, ring, wire_dtype):
    size = len(ring)
    ahead = size // 2
    behind = size - 1 - ahead
    blocks = part.reshape((size, part.shape[0] // size) + part.shape[1:])

    def block_at(offset):
        return blocks[(offset + ahead) % size]

    def to_wire(value):
        return value.astype(wire_dtype)

    result = block_at(0)
    ahead_value = to_wire(block_at(ahead)) if ahead else None
    behind_value = to_wire(block_at(-behind)) if behind else None
    for step in range(max(ahead, behind)):
        ahead_value, behind_value = paired_shift(
            ahead_value if step < ahead else None,
            behind_value if step < behind else None,
            axis,
            ring,
        )
        if step < ahead - 1:
            ahead_value = to_wire(ahead_value.astype(part.dtype) + block_at(ahead - step - 1))
        elif step == ahead - 1:
            result = result + ahead_value.astype(part.dtype)
        if step < behind - 1:
            behind_value = to_wire(behind_value.astype(part.dtype) + block_at(-behind + step + 1))
        elif step == behind - 1:
            result = result + behind_value.astype(part.dtype)
    return result


def per_device(
    tokens,
    cotangent,
    expert_ids,
    combine,
    gate_weight,
    up_weight,
    down_weight,
    moment1,
    moment2,
    round_k,
):
    local_experts = gate_weight.shape[1]
    devices_exp = lax.axis_size("exp")
    experts = local_experts * devices_exp
    my_exp = lax.axis_index("exp")

    ring = ring_order(devices_exp)
    use_ring = devices_exp <= RING_MAX

    def gather(value):
        if use_ring:
            return ring_all_gather(value, "exp", ring)
        return lax.all_gather(value, "exp", axis=0, tiled=True)

    def reduce_scatter(value):
        if use_ring:
            return ring_reduce_scatter(value, "exp", ring, jnp.bfloat16)
        return lax.psum_scatter(value, "exp", scatter_dimension=0, tiled=True)

    gate_matrix = gate_weight[0]
    up_matrix = up_weight[0]
    down_matrix = down_weight[0]

    def token_slice(tokens, cotangent, expert_ids, combine):
        token_count, model_width = tokens.shape
        weight_table = dense_weights(expert_ids, combine, experts)
        weight_rows = -(-(token_count * experts) // model_width)
        weight_rows = -(-weight_rows // 8) * 8
        weight_flat = jnp.pad(
            weight_table.reshape(-1), (0, weight_rows * model_width - token_count * experts)
        )
        packed_tokens = jnp.concatenate([tokens, weight_flat.reshape(weight_rows, model_width)])
        gathered = gather(packed_tokens[None])
        group_tokens = gathered[:, :token_count].reshape(devices_exp * token_count, model_width)
        group_weight = (
            gathered[:, token_count:]
            .reshape(devices_exp, -1)[:, : token_count * experts]
            .reshape(devices_exp * token_count, experts)
        )
        _, cotangent = lax.optimization_barrier((gathered, cotangent))
        group_cot = gather(cotangent)
        local_weight = lax.dynamic_slice_in_dim(
            group_weight, my_exp * local_experts, local_experts, axis=1
        ).astype(jnp.float32)
        local_weight = jnp.transpose(local_weight)[:, :, None]

        def chunk_pass(chunk_tokens, chunk_cot, chunk_weight):
            gate_value = jnp.einsum(
                "td,edh->eth", chunk_tokens, gate_matrix, preferred_element_type=jnp.float32
            )
            up_value = jnp.einsum(
                "td,edh->eth", chunk_tokens, up_matrix, preferred_element_type=jnp.float32
            )
            sigmoid_gate = jax.nn.sigmoid(gate_value)
            active = gate_value * sigmoid_gate
            hidden = (active * up_value).astype(jnp.bfloat16)
            expert_out = as_bf16(
                jnp.einsum("eth,ehd->etd", hidden, down_matrix, preferred_element_type=jnp.float32)
            )
            mixed_part = jnp.sum(chunk_weight * expert_out, axis=0)
            chunk_cot, mixed_part = lax.optimization_barrier((chunk_cot, mixed_part))
            slot_cot = (chunk_weight * chunk_cot.astype(jnp.float32)[None]).astype(jnp.bfloat16)
            hidden_cot = jnp.einsum(
                "etd,ehd->eth", slot_cot, down_matrix, preferred_element_type=jnp.float32
            )
            gate_cot = (
                hidden_cot * up_value * sigmoid_gate * (1.0 + gate_value * (1.0 - sigmoid_gate))
            ).astype(jnp.bfloat16)
            up_cot = (hidden_cot * active).astype(jnp.bfloat16)
            down_grad = jnp.einsum(
                "eth,etd->ehd", hidden, slot_cot, preferred_element_type=jnp.float32
            )
            gate_grad = jnp.einsum(
                "td,eth->edh", chunk_tokens, gate_cot, preferred_element_type=jnp.float32
            )
            up_grad = jnp.einsum(
                "td,eth->edh", chunk_tokens, up_cot, preferred_element_type=jnp.float32
            )
            input_cot = as_bf16(
                jnp.einsum("eth,edh->etd", gate_cot, gate_matrix, preferred_element_type=jnp.float32)
                + jnp.einsum("eth,edh->etd", up_cot, up_matrix, preferred_element_type=jnp.float32)
            )
            input_part = jnp.sum(input_cot, axis=0)
            return mixed_part, input_part, gate_grad, up_grad, down_grad

        group_count = group_tokens.shape[0]
        chunk = min(group_count, CHUNK_ROWS)
        chunks = group_count // chunk
        if chunks == 1:
            mixed_part, input_part, gate_grad, up_grad, down_grad = chunk_pass(
                group_tokens, group_cot, local_weight
            )
        else:

            def step(carry, packed):
                parts = chunk_pass(*packed)
                grads = tuple(acc + part for acc, part in zip(carry, parts[2:]))
                return grads, parts[:2]

            zeros = (
                jnp.zeros(gate_matrix.shape, jnp.float32),
                jnp.zeros(up_matrix.shape, jnp.float32),
                jnp.zeros(down_matrix.shape, jnp.float32),
            )
            packed = (
                group_tokens.reshape(chunks, chunk, -1),
                group_cot.reshape(chunks, chunk, -1),
                jnp.transpose(local_weight.reshape(local_experts, chunks, chunk, 1), (1, 0, 2, 3)),
            )
            (gate_grad, up_grad, down_grad), (mixed_parts, input_parts) = lax.scan(
                step, zeros, packed
            )
            mixed_part = mixed_parts.reshape(group_count, -1)
            input_part = input_parts.reshape(group_count, -1)
        mixed = reduce_scatter(mixed_part).astype(jnp.bfloat16)
        input_grad = reduce_scatter(input_part).astype(jnp.bfloat16)
        return mixed, input_grad, gate_grad, up_grad, down_grad

    slices = SLICES if use_ring else 1
    rows = tokens.shape[0] // slices
    results = [
        token_slice(
            tokens[s * rows : (s + 1) * rows],
            cotangent[s * rows : (s + 1) * rows],
            expert_ids[s * rows : (s + 1) * rows],
            combine[s * rows : (s + 1) * rows],
        )
        for s in range(slices)
    ]
    mixed = jnp.concatenate([r[0] for r in results])
    input_grad = jnp.concatenate([r[1] for r in results])
    gate_grad, up_grad, down_grad = results[0][2:]
    for r in results[1:]:
        gate_grad, up_grad, down_grad = gate_grad + r[2], up_grad + r[3], down_grad + r[4]
    gate_grad = gate_grad.astype(jnp.bfloat16)
    up_grad = up_grad.astype(jnp.bfloat16)

    peers = [shifted(down_weight, "rep", 1 << bit_index) for bit_index in range(ROUNDS)]
    peer_down = peers[0]
    for bit_index in range(1, ROUNDS):
        peer_down = jnp.where(round_k[0] == bit_index, peers[bit_index], peer_down)
    bias_one = 1.0 - beta_one**step_count
    bias_two = 1.0 - beta_two**step_count
    first = beta_one * moment1[0] + (1.0 - beta_one) * down_grad
    second = beta_two * moment2[0] + (1.0 - beta_two) * down_grad * down_grad
    own_down = down_matrix.astype(jnp.float32)
    averaged = (own_down + peer_down[0].astype(jnp.float32)) * 0.5
    update = first / bias_one / (jnp.sqrt(second / bias_two) + adam_eps)
    new_down = (averaged - learn_rate * (update + decay_rate * own_down)).astype(jnp.bfloat16)
    return (
        mixed,
        input_grad,
        gate_grad[None],
        up_grad[None],
        new_down[None],
        first[None],
        second[None],
    )


def solution(mesh):
    return jax.shard_map(
        per_device,
        mesh=mesh,
        in_specs=(
            P(("rep", "exp"), None),
            P(("rep", "exp"), None),
            P(("rep", "exp"), None),
            P(("rep", "exp"), None),
            P("rep", "exp", None, None),
            P("rep", "exp", None, None),
            P("rep", "exp", None, None),
            P("rep", "exp", None, None),
            P("rep", "exp", None, None),
            P("exp"),
        ),
        out_specs=(
            P(("rep", "exp"), None),
            P(("rep", "exp"), None),
            P("rep", "exp", None, None),
            P("rep", "exp", None, None),
            P("rep", "exp", None, None),
            P("rep", "exp", None, None),
            P("rep", "exp", None, None),
        ),
        check_vma=False,
    )
```

```python
import jax
import jax.numpy as jnp
from jax import lax
from jax.sharding import PartitionSpec as P

ROUNDS = 2
CHUNK_ROWS = 2048
RING_MAX = 8


beta_one = 0.9
beta_two = 0.999
learn_rate = 0.01
decay_rate = 0.1
adam_eps = 1e-08
step_count = 100.0


def shifted(value, axis, by):
    size = lax.axis_size(axis)
    return lax.ppermute(value, axis, [(i, (i + by) % size) for i in range(size)])


def as_bf16(value):
    return lax.reduce_precision(value, exponent_bits=8, mantissa_bits=7)


def dense_weights(expert_ids, combine, experts):
    expert_iota = jnp.arange(experts, dtype=jnp.int32)
    hit = expert_ids[:, :, None] == expert_iota[None, None, :]
    picked = jnp.where(hit, combine.astype(jnp.float32)[:, :, None], 0.0)
    return jnp.sum(picked, axis=1).astype(jnp.bfloat16)


def ring_order(size):
    return list(range(0, size, 2)) + list(range(size - 1 - size % 2, 0, -2))


def ring_positions(ring):
    position = [0] * len(ring)
    for place, device in enumerate(ring):
        position[device] = place
    return position


def ring_pairs(ring, step):
    size = len(ring)
    return [(ring[q], ring[(q + step) % size]) for q in range(size)]


def paired_shift(ahead_value, behind_value, axis, ring):
    if behind_value is None:
        return lax.ppermute(ahead_value, axis, ring_pairs(ring, 1)), None
    if ahead_value is None:
        return None, lax.ppermute(behind_value, axis, ring_pairs(ring, -1))
    ahead_value, behind_value = lax.optimization_barrier((ahead_value, behind_value))
    ahead_value = lax.ppermute(ahead_value, axis, ring_pairs(ring, 1))
    behind_value = lax.ppermute(behind_value, axis, ring_pairs(ring, -1))
    return lax.optimization_barrier((ahead_value, behind_value))


def ring_all_gather(shard, axis, ring):
    size = len(ring)
    ahead = size // 2
    behind = size - 1 - ahead
    got = {0: shard}
    ahead_value = shard
    behind_value = shard
    for step in range(max(ahead, behind)):
        ahead_value, behind_value = paired_shift(
            ahead_value if step < ahead else None,
            behind_value if step < behind else None,
            axis,
            ring,
        )
        if step < ahead:
            got[-(step + 1)] = ahead_value
        if step < behind:
            got[step + 1] = behind_value
    return jnp.concatenate([got[offset] for offset in range(-ahead, behind + 1)])


def ring_reduce_scatter(part, axis, ring, wire_dtype):
    size = len(ring)
    ahead = size // 2
    behind = size - 1 - ahead
    blocks = part.reshape((size, part.shape[0] // size) + part.shape[1:])

    def block_at(offset):
        return blocks[(offset + ahead) % size]

    def to_wire(value):
        return value.astype(wire_dtype)

    result = block_at(0)
    ahead_value = to_wire(block_at(ahead)) if ahead else None
    behind_value = to_wire(block_at(-behind)) if behind else None
    for step in range(max(ahead, behind)):
        ahead_value, behind_value = paired_shift(
            ahead_value if step < ahead else None,
            behind_value if step < behind else None,
            axis,
            ring,
        )
        if step < ahead - 1:
            ahead_value = to_wire(ahead_value.astype(part.dtype) + block_at(ahead - step - 1))
        elif step == ahead - 1:
            result = result + ahead_value.astype(part.dtype)
        if step < behind - 1:
            behind_value = to_wire(behind_value.astype(part.dtype) + block_at(-behind + step + 1))
        elif step == behind - 1:
            result = result + behind_value.astype(part.dtype)
    return result


def per_device(
    tokens,
    cotangent,
    expert_ids,
    combine,
    gate_weight,
    up_weight,
    down_weight,
    moment1,
    moment2,
    round_k,
):
    local_experts = gate_weight.shape[1]
    devices_exp = lax.axis_size("exp")
    experts = local_experts * devices_exp
    my_exp = lax.axis_index("exp")

    token_count, model_width = tokens.shape
    weight_table = dense_weights(expert_ids, combine, experts)
    weight_rows = -(-(token_count * experts) // model_width)
    weight_rows = -(-weight_rows // 8) * 8
    weight_flat = jnp.pad(
        weight_table.reshape(-1), (0, weight_rows * model_width - token_count * experts)
    )
    packed_tokens = jnp.concatenate([tokens, weight_flat.reshape(weight_rows, model_width)])
    ring = ring_order(devices_exp)
    use_ring = devices_exp <= RING_MAX

    def gather(value):
        if use_ring:
            return ring_all_gather(value, "exp", ring)
        return lax.all_gather(value, "exp", axis=0, tiled=True)

    def reduce_scatter(value):
        if use_ring:
            return ring_reduce_scatter(value, "exp", ring, jnp.bfloat16)
        return lax.psum_scatter(value, "exp", scatter_dimension=0, tiled=True)

    gathered = gather(packed_tokens[None])
    group_tokens = gathered[:, :token_count].reshape(devices_exp * token_count, model_width)
    group_weight = (
        gathered[:, token_count:]
        .reshape(devices_exp, -1)[:, : token_count * experts]
        .reshape(devices_exp * token_count, experts)
    )
    _, cotangent = lax.optimization_barrier((gathered, cotangent))
    group_cot = gather(cotangent)
    local_weight = lax.dynamic_slice_in_dim(
        group_weight, my_exp * local_experts, local_experts, axis=1
    ).astype(jnp.float32)
    local_weight = jnp.transpose(local_weight)[:, :, None]

    gate_matrix = gate_weight[0]
    up_matrix = up_weight[0]
    down_matrix = down_weight[0]

    def chunk_pass(chunk_tokens, chunk_cot, chunk_weight):
        gate_value = jnp.einsum(
            "td,edh->eth", chunk_tokens, gate_matrix, preferred_element_type=jnp.float32
        )
        up_value = jnp.einsum(
            "td,edh->eth", chunk_tokens, up_matrix, preferred_element_type=jnp.float32
        )
        sigmoid_gate = jax.nn.sigmoid(gate_value)
        active = gate_value * sigmoid_gate
        hidden = (active * up_value).astype(jnp.bfloat16)
        expert_out = as_bf16(
            jnp.einsum("eth,ehd->etd", hidden, down_matrix, preferred_element_type=jnp.float32)
        )
        mixed_part = jnp.sum(chunk_weight * expert_out, axis=0)
        chunk_cot, mixed_part = lax.optimization_barrier((chunk_cot, mixed_part))
        slot_cot = (chunk_weight * chunk_cot.astype(jnp.float32)[None]).astype(jnp.bfloat16)
        hidden_cot = jnp.einsum(
            "etd,ehd->eth", slot_cot, down_matrix, preferred_element_type=jnp.float32
        )
        gate_cot = (
            hidden_cot * up_value * sigmoid_gate * (1.0 + gate_value * (1.0 - sigmoid_gate))
        ).astype(jnp.bfloat16)
        up_cot = (hidden_cot * active).astype(jnp.bfloat16)
        down_grad = jnp.einsum(
            "eth,etd->ehd", hidden, slot_cot, preferred_element_type=jnp.float32
        )
        gate_grad = jnp.einsum(
            "td,eth->edh", chunk_tokens, gate_cot, preferred_element_type=jnp.float32
        )
        up_grad = jnp.einsum(
            "td,eth->edh", chunk_tokens, up_cot, preferred_element_type=jnp.float32
        )
        input_cot = as_bf16(
            jnp.einsum("eth,edh->etd", gate_cot, gate_matrix, preferred_element_type=jnp.float32)
            + jnp.einsum("eth,edh->etd", up_cot, up_matrix, preferred_element_type=jnp.float32)
        )
        input_part = jnp.sum(input_cot, axis=0)
        return mixed_part, input_part, gate_grad, up_grad, down_grad

    group_count = group_tokens.shape[0]
    chunk = min(group_count, CHUNK_ROWS)
    chunks = group_count // chunk
    if chunks == 1:
        mixed_part, input_part, gate_grad, up_grad, down_grad = chunk_pass(
            group_tokens, group_cot, local_weight
        )
    else:

        def step(carry, packed):
            parts = chunk_pass(*packed)
            grads = tuple(acc + part for acc, part in zip(carry, parts[2:]))
            return grads, parts[:2]

        zeros = (
            jnp.zeros(gate_matrix.shape, jnp.float32),
            jnp.zeros(up_matrix.shape, jnp.float32),
            jnp.zeros(down_matrix.shape, jnp.float32),
        )
        packed = (
            group_tokens.reshape(chunks, chunk, -1),
            group_cot.reshape(chunks, chunk, -1),
            jnp.transpose(local_weight.reshape(local_experts, chunks, chunk, 1), (1, 0, 2, 3)),
        )
        (gate_grad, up_grad, down_grad), (mixed_parts, input_parts) = lax.scan(
            step, zeros, packed
        )
        mixed_part = mixed_parts.reshape(group_count, -1)
        input_part = input_parts.reshape(group_count, -1)
    gate_grad = gate_grad.astype(jnp.bfloat16)
    up_grad = up_grad.astype(jnp.bfloat16)
    if use_ring:
        ahead = devices_exp // 2
        position = jnp.asarray(ring_positions(ring), jnp.int32)
        block_order = (position - position[my_exp] + ahead) % devices_exp
        mixed_blocks = mixed_part.reshape((devices_exp, -1) + mixed_part.shape[1:])
        mixed_part = jnp.take(mixed_blocks, block_order, axis=0).reshape(mixed_part.shape)
        mixed_part = mixed_part.astype(jnp.bfloat16)
    mixed = lax.psum_scatter(mixed_part, "exp", scatter_dimension=0, tiled=True).astype(
        jnp.bfloat16
    )
    input_grad = reduce_scatter(input_part).astype(jnp.bfloat16)

    peers = [shifted(down_weight, "rep", 1 << bit_index) for bit_index in range(ROUNDS)]
    peer_down = peers[0]
    for bit_index in range(1, ROUNDS):
        peer_down = jnp.where(round_k[0] == bit_index, peers[bit_index], peer_down)
    bias_one = 1.0 - beta_one**step_count
    bias_two = 1.0 - beta_two**step_count
    first = beta_one * moment1[0] + (1.0 - beta_one) * down_grad
    second = beta_two * moment2[0] + (1.0 - beta_two) * down_grad * down_grad
    own_down = down_matrix.astype(jnp.float32)
    averaged = (own_down + peer_down[0].astype(jnp.float32)) * 0.5
    update = first / bias_one / (jnp.sqrt(second / bias_two) + adam_eps)
    new_down = (averaged - learn_rate * (update + decay_rate * own_down)).astype(jnp.bfloat16)
    return (
        mixed,
        input_grad,
        gate_grad[None],
        up_grad[None],
        new_down[None],
        first[None],
        second[None],
    )


def solution(mesh):
    return jax.shard_map(
        per_device,
        mesh=mesh,
        in_specs=(
            P(("rep", "exp"), None),
            P(("rep", "exp"), None),
            P(("rep", "exp"), None),
            P(("rep", "exp"), None),
            P("rep", "exp", None, None),
            P("rep", "exp", None, None),
            P("rep", "exp", None, None),
            P("rep", "exp", None, None),
            P("rep", "exp", None, None),
            P("exp"),
        ),
        out_specs=(
            P(("rep", "exp"), None),
            P(("rep", "exp"), None),
            P("rep", "exp", None, None),
            P("rep", "exp", None, None),
            P("rep", "exp", None, None),
            P("rep", "exp", None, None),
            P("rep", "exp", None, None),
        ),
        check_vma=False,
    )
```

```python
import jax
import jax.numpy as jnp
from jax import lax
from jax.sharding import PartitionSpec as P

ROUNDS = 2
CHUNK_ROWS = 2048
RING_MAX = 8


beta_one = 0.9
beta_two = 0.999
learn_rate = 0.01
decay_rate = 0.1
adam_eps = 1e-08
step_count = 100.0


def shifted(value, axis, by):
    size = lax.axis_size(axis)
    return lax.ppermute(value, axis, [(i, (i + by) % size) for i in range(size)])


def as_bf16(value):
    return lax.reduce_precision(value, exponent_bits=8, mantissa_bits=7)


def dense_weights(expert_ids, combine, experts):
    expert_iota = jnp.arange(experts, dtype=jnp.int32)
    hit = expert_ids[:, :, None] == expert_iota[None, None, :]
    picked = jnp.where(hit, combine.astype(jnp.float32)[:, :, None], 0.0)
    return jnp.sum(picked, axis=1).astype(jnp.bfloat16)


def ring_order(size):
    return list(range(0, size, 2)) + list(range(size - 1 - size % 2, 0, -2))


def ring_pairs(ring, step):
    size = len(ring)
    return [(ring[q], ring[(q + step) % size]) for q in range(size)]


def paired_shift(ahead_value, behind_value, axis, ring):
    if behind_value is None:
        return lax.ppermute(ahead_value, axis, ring_pairs(ring, 1)), None
    if ahead_value is None:
        return None, lax.ppermute(behind_value, axis, ring_pairs(ring, -1))
    ahead_value, behind_value = lax.optimization_barrier((ahead_value, behind_value))
    ahead_value = lax.ppermute(ahead_value, axis, ring_pairs(ring, 1))
    behind_value = lax.ppermute(behind_value, axis, ring_pairs(ring, -1))
    return lax.optimization_barrier((ahead_value, behind_value))


def ring_all_gather(shard, axis, ring):
    size = len(ring)
    ahead = size // 2
    behind = size - 1 - ahead
    gathered = jnp.zeros((size,) + shard.shape, shard.dtype)
    gathered = lax.dynamic_update_index_in_dim(gathered, shard, ahead, axis=0)
    ahead_value = shard
    behind_value = shard
    for step in range(max(ahead, behind)):
        ahead_value, behind_value = paired_shift(
            ahead_value if step < ahead else None,
            behind_value if step < behind else None,
            axis,
            ring,
        )
        if step < ahead:
            gathered = lax.dynamic_update_index_in_dim(
                gathered, ahead_value, ahead - step - 1, axis=0
            )
        if step < behind:
            gathered = lax.dynamic_update_index_in_dim(
                gathered, behind_value, ahead + step + 1, axis=0
            )
    return gathered.reshape((size * shard.shape[0],) + shard.shape[1:])


def ring_reduce_scatter(part, axis, ring, wire_dtype):
    size = len(ring)
    ahead = size // 2
    behind = size - 1 - ahead
    blocks = part.reshape((size, part.shape[0] // size) + part.shape[1:])

    def block_at(offset):
        return blocks[(offset + ahead) % size]

    def to_wire(value):
        return value.astype(wire_dtype)

    result = block_at(0)
    ahead_value = to_wire(block_at(ahead)) if ahead else None
    behind_value = to_wire(block_at(-behind)) if behind else None
    for step in range(max(ahead, behind)):
        ahead_value, behind_value = paired_shift(
            ahead_value if step < ahead else None,
            behind_value if step < behind else None,
            axis,
            ring,
        )
        if step < ahead - 1:
            ahead_value = to_wire(ahead_value.astype(part.dtype) + block_at(ahead - step - 1))
        elif step == ahead - 1:
            result = result + ahead_value.astype(part.dtype)
        if step < behind - 1:
            behind_value = to_wire(behind_value.astype(part.dtype) + block_at(-behind + step + 1))
        elif step == behind - 1:
            result = result + behind_value.astype(part.dtype)
    return result


def per_device(
    tokens,
    cotangent,
    expert_ids,
    combine,
    gate_weight,
    up_weight,
    down_weight,
    moment1,
    moment2,
    round_k,
):
    local_experts = gate_weight.shape[1]
    devices_exp = lax.axis_size("exp")
    experts = local_experts * devices_exp
    my_exp = lax.axis_index("exp")

    token_count, model_width = tokens.shape
    weight_table = dense_weights(expert_ids, combine, experts)
    weight_rows = -(-(token_count * experts) // model_width)
    weight_rows = -(-weight_rows // 8) * 8
    weight_flat = jnp.pad(
        weight_table.reshape(-1), (0, weight_rows * model_width - token_count * experts)
    )
    packed_tokens = jnp.concatenate([tokens, weight_flat.reshape(weight_rows, model_width)])
    ring = ring_order(devices_exp)
    use_ring = devices_exp <= RING_MAX

    def gather(value):
        if use_ring:
            return ring_all_gather(value, "exp", ring)
        return lax.all_gather(value, "exp", axis=0, tiled=True)

    def reduce_scatter(value):
        if use_ring:
            return ring_reduce_scatter(value, "exp", ring, jnp.bfloat16)
        return lax.psum_scatter(value, "exp", scatter_dimension=0, tiled=True)

    gathered = gather(packed_tokens[None])
    group_tokens = gathered[:, :token_count].reshape(devices_exp * token_count, model_width)
    group_weight = (
        gathered[:, token_count:]
        .reshape(devices_exp, -1)[:, : token_count * experts]
        .reshape(devices_exp * token_count, experts)
    )
    _, cotangent = lax.optimization_barrier((gathered, cotangent))
    group_cot = gather(cotangent)
    local_weight = lax.dynamic_slice_in_dim(
        group_weight, my_exp * local_experts, local_experts, axis=1
    ).astype(jnp.float32)
    local_weight = jnp.transpose(local_weight)[:, :, None]

    gate_matrix = gate_weight[0]
    up_matrix = up_weight[0]
    down_matrix = down_weight[0]

    def chunk_pass(chunk_tokens, chunk_cot, chunk_weight):
        gate_value = jnp.einsum(
            "td,edh->eth", chunk_tokens, gate_matrix, preferred_element_type=jnp.float32
        )
        up_value = jnp.einsum(
            "td,edh->eth", chunk_tokens, up_matrix, preferred_element_type=jnp.float32
        )
        sigmoid_gate = jax.nn.sigmoid(gate_value)
        active = gate_value * sigmoid_gate
        hidden = (active * up_value).astype(jnp.bfloat16)
        expert_out = as_bf16(
            jnp.einsum("eth,ehd->etd", hidden, down_matrix, preferred_element_type=jnp.float32)
        )
        mixed_part = jnp.sum(chunk_weight * expert_out, axis=0)
        chunk_cot, mixed_part = lax.optimization_barrier((chunk_cot, mixed_part))
        slot_cot = (chunk_weight * chunk_cot.astype(jnp.float32)[None]).astype(jnp.bfloat16)
        hidden_cot = jnp.einsum(
            "etd,ehd->eth", slot_cot, down_matrix, preferred_element_type=jnp.float32
        )
        gate_cot = (
            hidden_cot * up_value * sigmoid_gate * (1.0 + gate_value * (1.0 - sigmoid_gate))
        ).astype(jnp.bfloat16)
        up_cot = (hidden_cot * active).astype(jnp.bfloat16)
        down_grad = jnp.einsum(
            "eth,etd->ehd", hidden, slot_cot, preferred_element_type=jnp.float32
        )
        gate_grad = jnp.einsum(
            "td,eth->edh", chunk_tokens, gate_cot, preferred_element_type=jnp.float32
        )
        up_grad = jnp.einsum(
            "td,eth->edh", chunk_tokens, up_cot, preferred_element_type=jnp.float32
        )
        input_cot = as_bf16(
            jnp.einsum("eth,edh->etd", gate_cot, gate_matrix, preferred_element_type=jnp.float32)
            + jnp.einsum("eth,edh->etd", up_cot, up_matrix, preferred_element_type=jnp.float32)
        )
        input_part = jnp.sum(input_cot, axis=0)
        return mixed_part, input_part, gate_grad, up_grad, down_grad

    group_count = group_tokens.shape[0]
    chunk = min(group_count, CHUNK_ROWS)
    chunks = group_count // chunk
    if chunks == 1:
        mixed_part, input_part, gate_grad, up_grad, down_grad = chunk_pass(
            group_tokens, group_cot, local_weight
        )
    else:

        def step(carry, packed):
            parts = chunk_pass(*packed)
            grads = tuple(acc + part for acc, part in zip(carry, parts[2:]))
            return grads, parts[:2]

        zeros = (
            jnp.zeros(gate_matrix.shape, jnp.float32),
            jnp.zeros(up_matrix.shape, jnp.float32),
            jnp.zeros(down_matrix.shape, jnp.float32),
        )
        packed = (
            group_tokens.reshape(chunks, chunk, -1),
            group_cot.reshape(chunks, chunk, -1),
            jnp.transpose(local_weight.reshape(local_experts, chunks, chunk, 1), (1, 0, 2, 3)),
        )
        (gate_grad, up_grad, down_grad), (mixed_parts, input_parts) = lax.scan(
            step, zeros, packed
        )
        mixed_part = mixed_parts.reshape(group_count, -1)
        input_part = input_parts.reshape(group_count, -1)
    gate_grad = gate_grad.astype(jnp.bfloat16)
    up_grad = up_grad.astype(jnp.bfloat16)
    mixed = reduce_scatter(mixed_part).astype(jnp.bfloat16)
    input_grad = reduce_scatter(input_part).astype(jnp.bfloat16)

    peers = [shifted(down_weight, "rep", 1 << bit_index) for bit_index in range(ROUNDS)]
    peer_down = peers[0]
    for bit_index in range(1, ROUNDS):
        peer_down = jnp.where(round_k[0] == bit_index, peers[bit_index], peer_down)
    bias_one = 1.0 - beta_one**step_count
    bias_two = 1.0 - beta_two**step_count
    first = beta_one * moment1[0] + (1.0 - beta_one) * down_grad
    second = beta_two * moment2[0] + (1.0 - beta_two) * down_grad * down_grad
    own_down = down_matrix.astype(jnp.float32)
    averaged = (own_down + peer_down[0].astype(jnp.float32)) * 0.5
    update = first / bias_one / (jnp.sqrt(second / bias_two) + adam_eps)
    new_down = (averaged - learn_rate * (update + decay_rate * own_down)).astype(jnp.bfloat16)
    return (
        mixed,
        input_grad,
        gate_grad[None],
        up_grad[None],
        new_down[None],
        first[None],
        second[None],
    )


def solution(mesh):
    return jax.shard_map(
        per_device,
        mesh=mesh,
        in_specs=(
            P(("rep", "exp"), None),
            P(("rep", "exp"), None),
            P(("rep", "exp"), None),
            P(("rep", "exp"), None),
            P("rep", "exp", None, None),
            P("rep", "exp", None, None),
            P("rep", "exp", None, None),
            P("rep", "exp", None, None),
            P("rep", "exp", None, None),
            P("exp"),
        ),
        out_specs=(
            P(("rep", "exp"), None),
            P(("rep", "exp"), None),
            P("rep", "exp", None, None),
            P("rep", "exp", None, None),
            P("rep", "exp", None, None),
            P("rep", "exp", None, None),
            P("rep", "exp", None, None),
        ),
        check_vma=False,
    )
```

```python
import jax
import jax.numpy as jnp
from jax import lax
from jax.sharding import PartitionSpec as P

ROUNDS = 2
CHUNK_ROWS = 2048
RING_MAX = 8


beta_one = 0.9
beta_two = 0.999
learn_rate = 0.01
decay_rate = 0.1
adam_eps = 1e-08
step_count = 100.0


def shifted(value, axis, by):
    size = lax.axis_size(axis)
    return lax.ppermute(value, axis, [(i, (i + by) % size) for i in range(size)])


def as_bf16(value):
    return lax.reduce_precision(value, exponent_bits=8, mantissa_bits=7)


def dense_weights(expert_ids, combine, experts):
    expert_iota = jnp.arange(experts, dtype=jnp.int32)
    hit = expert_ids[:, :, None] == expert_iota[None, None, :]
    picked = jnp.where(hit, combine.astype(jnp.float32)[:, :, None], 0.0)
    return jnp.sum(picked, axis=1).astype(jnp.bfloat16)


def ring_order(size):
    return list(range(0, size, 2)) + list(range(size - 1 - size % 2, 0, -2))


def ring_pairs(ring, step):
    size = len(ring)
    return [(ring[q], ring[(q + step) % size]) for q in range(size)]


def paired_shift(ahead_value, behind_value, axis, ring):
    if behind_value is None:
        return lax.ppermute(ahead_value, axis, ring_pairs(ring, 1)), None
    if ahead_value is None:
        return None, lax.ppermute(behind_value, axis, ring_pairs(ring, -1))
    ahead_value, behind_value = lax.optimization_barrier((ahead_value, behind_value))
    ahead_value = lax.ppermute(ahead_value, axis, ring_pairs(ring, 1))
    behind_value = lax.ppermute(behind_value, axis, ring_pairs(ring, -1))
    return lax.optimization_barrier((ahead_value, behind_value))


def ring_all_gather(shard, axis, ring):
    size = len(ring)
    ahead = size // 2
    behind = size - 1 - ahead
    got = {0: shard}
    ahead_value = shard
    behind_value = shard
    for step in range(max(ahead, behind)):
        ahead_value, behind_value = paired_shift(
            ahead_value if step < ahead else None,
            behind_value if step < behind else None,
            axis,
            ring,
        )
        if step < ahead:
            got[-(step + 1)] = ahead_value
        if step < behind:
            got[step + 1] = behind_value
    return jnp.concatenate([got[offset] for offset in range(-ahead, behind + 1)])


def ring_reduce_scatter(part, axis, ring, wire_dtype):
    size = len(ring)
    ahead = size // 2
    behind = size - 1 - ahead
    blocks = part.reshape((size, part.shape[0] // size) + part.shape[1:])

    def block_at(offset):
        return blocks[(offset + ahead) % size]

    def to_wire(value):
        return value.astype(wire_dtype)

    result = block_at(0)
    ahead_value = to_wire(block_at(ahead)) if ahead else None
    behind_value = to_wire(block_at(-behind)) if behind else None
    for step in range(max(ahead, behind)):
        ahead_value, behind_value = paired_shift(
            ahead_value if step < ahead else None,
            behind_value if step < behind else None,
            axis,
            ring,
        )
        if step < ahead - 1:
            ahead_value = to_wire(ahead_value.astype(part.dtype) + block_at(ahead - step - 1))
        elif step == ahead - 1:
            result = result + ahead_value.astype(part.dtype)
        if step < behind - 1:
            behind_value = to_wire(behind_value.astype(part.dtype) + block_at(-behind + step + 1))
        elif step == behind - 1:
            result = result + behind_value.astype(part.dtype)
    return result


def per_device(
    tokens,
    cotangent,
    expert_ids,
    combine,
    gate_weight,
    up_weight,
    down_weight,
    moment1,
    moment2,
    round_k,
):
    local_experts = gate_weight.shape[1]
    devices_exp = lax.axis_size("exp")
    experts = local_experts * devices_exp
    my_exp = lax.axis_index("exp")

    token_count, model_width = tokens.shape
    weight_table = dense_weights(expert_ids, combine, experts)
    weight_rows = -(-(token_count * experts) // model_width)
    weight_rows = -(-weight_rows // 8) * 8
    weight_flat = jnp.pad(
        weight_table.reshape(-1), (0, weight_rows * model_width - token_count * experts)
    )
    packed_tokens = jnp.concatenate([tokens, weight_flat.reshape(weight_rows, model_width)])
    ring = ring_order(devices_exp)
    use_ring = devices_exp <= RING_MAX

    def gather(value):
        if use_ring:
            return ring_all_gather(value, "exp", ring)
        return lax.all_gather(value, "exp", axis=0, tiled=True)

    def reduce_scatter(value):
        if use_ring:
            return ring_reduce_scatter(value, "exp", ring, jnp.bfloat16)
        return lax.psum_scatter(value, "exp", scatter_dimension=0, tiled=True)

    gathered = gather(packed_tokens[None])
    group_tokens = gathered[:, :token_count].reshape(devices_exp * token_count, model_width)
    group_weight = (
        gathered[:, token_count:]
        .reshape(devices_exp, -1)[:, : token_count * experts]
        .reshape(devices_exp * token_count, experts)
    )
    _, cotangent = lax.optimization_barrier((gathered, cotangent))
    group_cot = gather(cotangent)
    local_weight = lax.dynamic_slice_in_dim(
        group_weight, my_exp * local_experts, local_experts, axis=1
    ).astype(jnp.float32)
    local_weight = jnp.transpose(local_weight)[:, :, None]

    gate_matrix = gate_weight[0]
    up_matrix = up_weight[0]
    down_matrix = down_weight[0]

    hidden_width = gate_matrix.shape[2]
    joint_matrix = jnp.concatenate([gate_matrix, up_matrix], axis=2)

    def chunk_pass(chunk_tokens, chunk_cot, chunk_weight):
        gate_value = jnp.einsum(
            "td,edh->eth", chunk_tokens, gate_matrix, preferred_element_type=jnp.float32
        )
        up_value = jnp.einsum(
            "td,edh->eth", chunk_tokens, up_matrix, preferred_element_type=jnp.float32
        )
        sigmoid_gate = jax.nn.sigmoid(gate_value)
        active = gate_value * sigmoid_gate
        hidden = (active * up_value).astype(jnp.bfloat16)
        expert_out = as_bf16(
            jnp.einsum("eth,ehd->etd", hidden, down_matrix, preferred_element_type=jnp.float32)
        )
        mixed_part = jnp.sum(chunk_weight * expert_out, axis=0)
        chunk_cot, mixed_part = lax.optimization_barrier((chunk_cot, mixed_part))
        slot_cot = (chunk_weight * chunk_cot.astype(jnp.float32)[None]).astype(jnp.bfloat16)
        hidden_cot = jnp.einsum(
            "etd,ehd->eth", slot_cot, down_matrix, preferred_element_type=jnp.float32
        )
        gate_cot = (
            hidden_cot * up_value * sigmoid_gate * (1.0 + gate_value * (1.0 - sigmoid_gate))
        ).astype(jnp.bfloat16)
        up_cot = (hidden_cot * active).astype(jnp.bfloat16)
        down_grad = jnp.einsum(
            "eth,etd->ehd", hidden, slot_cot, preferred_element_type=jnp.float32
        )
        joint_cot = jnp.concatenate([gate_cot, up_cot], axis=2)
        joint_grad = jnp.einsum(
            "td,eth->edh", chunk_tokens, joint_cot, preferred_element_type=jnp.float32
        )
        gate_grad = joint_grad[..., :hidden_width]
        up_grad = joint_grad[..., hidden_width:]
        input_cot = as_bf16(
            jnp.einsum("eth,edh->etd", joint_cot, joint_matrix, preferred_element_type=jnp.float32)
        )
        input_part = jnp.sum(input_cot, axis=0)
        return mixed_part, input_part, gate_grad, up_grad, down_grad

    group_count = group_tokens.shape[0]
    chunk = min(group_count, CHUNK_ROWS)
    chunks = group_count // chunk
    if chunks == 1:
        mixed_part, input_part, gate_grad, up_grad, down_grad = chunk_pass(
            group_tokens, group_cot, local_weight
        )
    else:

        def step(carry, packed):
            parts = chunk_pass(*packed)
            grads = tuple(acc + part for acc, part in zip(carry, parts[2:]))
            return grads, parts[:2]

        zeros = (
            jnp.zeros(gate_matrix.shape, jnp.float32),
            jnp.zeros(up_matrix.shape, jnp.float32),
            jnp.zeros(down_matrix.shape, jnp.float32),
        )
        packed = (
            group_tokens.reshape(chunks, chunk, -1),
            group_cot.reshape(chunks, chunk, -1),
            jnp.transpose(local_weight.reshape(local_experts, chunks, chunk, 1), (1, 0, 2, 3)),
        )
        (gate_grad, up_grad, down_grad), (mixed_parts, input_parts) = lax.scan(
            step, zeros, packed
        )
        mixed_part = mixed_parts.reshape(group_count, -1)
        input_part = input_parts.reshape(group_count, -1)
    gate_grad = gate_grad.astype(jnp.bfloat16)
    up_grad = up_grad.astype(jnp.bfloat16)
    mixed = reduce_scatter(mixed_part).astype(jnp.bfloat16)
    input_grad = reduce_scatter(input_part).astype(jnp.bfloat16)

    peers = [shifted(down_weight, "rep", 1 << bit_index) for bit_index in range(ROUNDS)]
    peer_down = peers[0]
    for bit_index in range(1, ROUNDS):
        peer_down = jnp.where(round_k[0] == bit_index, peers[bit_index], peer_down)
    bias_one = 1.0 - beta_one**step_count
    bias_two = 1.0 - beta_two**step_count
    first = beta_one * moment1[0] + (1.0 - beta_one) * down_grad
    second = beta_two * moment2[0] + (1.0 - beta_two) * down_grad * down_grad
    own_down = down_matrix.astype(jnp.float32)
    averaged = (own_down + peer_down[0].astype(jnp.float32)) * 0.5
    update = first / bias_one / (jnp.sqrt(second / bias_two) + adam_eps)
    new_down = (averaged - learn_rate * (update + decay_rate * own_down)).astype(jnp.bfloat16)
    return (
        mixed,
        input_grad,
        gate_grad[None],
        up_grad[None],
        new_down[None],
        first[None],
        second[None],
    )


def solution(mesh):
    return jax.shard_map(
        per_device,
        mesh=mesh,
        in_specs=(
            P(("rep", "exp"), None),
            P(("rep", "exp"), None),
            P(("rep", "exp"), None),
            P(("rep", "exp"), None),
            P("rep", "exp", None, None),
            P("rep", "exp", None, None),
            P("rep", "exp", None, None),
            P("rep", "exp", None, None),
            P("rep", "exp", None, None),
            P("exp"),
        ),
        out_specs=(
            P(("rep", "exp"), None),
            P(("rep", "exp"), None),
            P("rep", "exp", None, None),
            P("rep", "exp", None, None),
            P("rep", "exp", None, None),
            P("rep", "exp", None, None),
            P("rep", "exp", None, None),
        ),
        check_vma=False,
    )
```

```python
import jax
import jax.numpy as jnp
from jax import lax
from jax.sharding import PartitionSpec as P

ROUNDS = 2
CHUNK_ROWS = 2048
RING_MAX = 8


beta_one = 0.9
beta_two = 0.999
learn_rate = 0.01
decay_rate = 0.1
adam_eps = 1e-08
step_count = 100.0


def shifted(value, axis, by):
    size = lax.axis_size(axis)
    return lax.ppermute(value, axis, [(i, (i + by) % size) for i in range(size)])


def as_bf16(value):
    return lax.reduce_precision(value, exponent_bits=8, mantissa_bits=7)


def dense_weights(expert_ids, combine, experts):
    expert_iota = jnp.arange(experts, dtype=jnp.int32)
    hit = expert_ids[:, :, None] == expert_iota[None, None, :]
    picked = jnp.where(hit, combine.astype(jnp.float32)[:, :, None], 0.0)
    return jnp.sum(picked, axis=1).astype(jnp.bfloat16)


def ring_order(size):
    return list(range(0, size, 2)) + list(range(size - 1 - size % 2, 0, -2))


def ring_pairs(ring, step):
    size = len(ring)
    return [(ring[q], ring[(q + step) % size]) for q in range(size)]


def paired_shift(ahead_value, behind_value, axis, ring):
    if behind_value is None:
        return lax.ppermute(ahead_value, axis, ring_pairs(ring, 1)), None
    if ahead_value is None:
        return None, lax.ppermute(behind_value, axis, ring_pairs(ring, -1))
    ahead_value, behind_value = lax.optimization_barrier((ahead_value, behind_value))
    ahead_value = lax.ppermute(ahead_value, axis, ring_pairs(ring, 1))
    behind_value = lax.ppermute(behind_value, axis, ring_pairs(ring, -1))
    return lax.optimization_barrier((ahead_value, behind_value))


def ring_all_gather(shard, axis, ring):
    size = len(ring)
    ahead = size // 2
    behind = size - 1 - ahead
    got = {0: shard}
    ahead_value = shard
    behind_value = shard
    for step in range(max(ahead, behind)):
        ahead_value, behind_value = paired_shift(
            ahead_value if step < ahead else None,
            behind_value if step < behind else None,
            axis,
            ring,
        )
        if step < ahead:
            got[-(step + 1)] = ahead_value
        if step < behind:
            got[step + 1] = behind_value
    return jnp.concatenate([got[offset] for offset in range(-ahead, behind + 1)])


def ring_reduce_scatter(part, axis, ring, wire_dtype):
    size = len(ring)
    ahead = size // 2
    behind = size - 1 - ahead
    blocks = part.reshape((size, part.shape[0] // size) + part.shape[1:])

    def block_at(offset):
        return blocks[(offset + ahead) % size]

    def to_wire(value):
        return value.astype(wire_dtype)

    result = block_at(0)
    ahead_value = to_wire(block_at(ahead)) if ahead else None
    behind_value = to_wire(block_at(-behind)) if behind else None
    for step in range(max(ahead, behind)):
        ahead_value, behind_value = paired_shift(
            ahead_value if step < ahead else None,
            behind_value if step < behind else None,
            axis,
            ring,
        )
        if step < ahead - 1:
            ahead_value = to_wire(ahead_value.astype(part.dtype) + block_at(ahead - step - 1))
        elif step == ahead - 1:
            result = result + ahead_value.astype(part.dtype)
        if step < behind - 1:
            behind_value = to_wire(behind_value.astype(part.dtype) + block_at(-behind + step + 1))
        elif step == behind - 1:
            result = result + behind_value.astype(part.dtype)
    return result


def per_device(
    tokens,
    cotangent,
    expert_ids,
    combine,
    gate_weight,
    up_weight,
    down_weight,
    moment1,
    moment2,
    round_k,
):
    local_experts = gate_weight.shape[1]
    devices_exp = lax.axis_size("exp")
    experts = local_experts * devices_exp
    my_exp = lax.axis_index("exp")

    token_count, model_width = tokens.shape
    weight_table = dense_weights(expert_ids, combine, experts)
    weight_rows = -(-(token_count * experts) // model_width)
    weight_rows = -(-weight_rows // 8) * 8
    weight_flat = jnp.pad(
        weight_table.reshape(-1), (0, weight_rows * model_width - token_count * experts)
    )
    packed_tokens = jnp.concatenate([tokens, weight_flat.reshape(weight_rows, model_width)])
    ring = ring_order(devices_exp)
    use_ring = devices_exp <= RING_MAX

    def gather(value):
        if use_ring:
            return ring_all_gather(value, "exp", ring)
        return lax.all_gather(value, "exp", axis=0, tiled=True)

    def reduce_scatter(value):
        if use_ring:
            return ring_reduce_scatter(value, "exp", ring, jnp.bfloat16)
        return lax.psum_scatter(value, "exp", scatter_dimension=0, tiled=True)

    gathered = gather(packed_tokens[None])
    group_tokens = gathered[:, :token_count].reshape(devices_exp * token_count, model_width)
    group_weight = (
        gathered[:, token_count:]
        .reshape(devices_exp, -1)[:, : token_count * experts]
        .reshape(devices_exp * token_count, experts)
    )
    _, cotangent = lax.optimization_barrier((gathered, cotangent))
    group_cot = gather(cotangent)
    local_weight = lax.dynamic_slice_in_dim(
        group_weight, my_exp * local_experts, local_experts, axis=1
    ).astype(jnp.float32)
    local_weight = jnp.transpose(local_weight)[:, :, None]

    gate_matrix = gate_weight[0]
    up_matrix = up_weight[0]
    down_matrix = down_weight[0]

    hidden_width = gate_matrix.shape[2]
    joint_matrix = jnp.concatenate([gate_matrix, up_matrix], axis=2)

    def chunk_pass(chunk_tokens, chunk_cot, chunk_weight):
        joint_value = jnp.einsum(
            "td,edh->eth", chunk_tokens, joint_matrix, preferred_element_type=jnp.float32
        )
        gate_value = joint_value[..., :hidden_width]
        up_value = joint_value[..., hidden_width:]
        sigmoid_gate = jax.nn.sigmoid(gate_value)
        active = gate_value * sigmoid_gate
        hidden = (active * up_value).astype(jnp.bfloat16)
        expert_out = as_bf16(
            jnp.einsum("eth,ehd->etd", hidden, down_matrix, preferred_element_type=jnp.float32)
        )
        mixed_part = jnp.sum(chunk_weight * expert_out, axis=0)
        chunk_cot, mixed_part = lax.optimization_barrier((chunk_cot, mixed_part))
        slot_cot = (chunk_weight * chunk_cot.astype(jnp.float32)[None]).astype(jnp.bfloat16)
        hidden_cot = jnp.einsum(
            "etd,ehd->eth", slot_cot, down_matrix, preferred_element_type=jnp.float32
        )
        gate_cot = (
            hidden_cot * up_value * sigmoid_gate * (1.0 + gate_value * (1.0 - sigmoid_gate))
        ).astype(jnp.bfloat16)
        up_cot = (hidden_cot * active).astype(jnp.bfloat16)
        down_grad = jnp.einsum(
            "eth,etd->ehd", hidden, slot_cot, preferred_element_type=jnp.float32
        )
        joint_cot = jnp.concatenate([gate_cot, up_cot], axis=2)
        joint_grad = jnp.einsum(
            "td,eth->edh", chunk_tokens, joint_cot, preferred_element_type=jnp.float32
        )
        gate_grad = joint_grad[..., :hidden_width]
        up_grad = joint_grad[..., hidden_width:]
        input_cot = as_bf16(
            jnp.einsum("eth,edh->etd", joint_cot, joint_matrix, preferred_element_type=jnp.float32)
        )
        input_part = jnp.sum(input_cot, axis=0)
        return mixed_part, input_part, gate_grad, up_grad, down_grad

    group_count = group_tokens.shape[0]
    chunk = min(group_count, CHUNK_ROWS)
    chunks = group_count // chunk
    if chunks == 1:
        mixed_part, input_part, gate_grad, up_grad, down_grad = chunk_pass(
            group_tokens, group_cot, local_weight
        )
    else:

        def step(carry, packed):
            parts = chunk_pass(*packed)
            grads = tuple(acc + part for acc, part in zip(carry, parts[2:]))
            return grads, parts[:2]

        zeros = (
            jnp.zeros(gate_matrix.shape, jnp.float32),
            jnp.zeros(up_matrix.shape, jnp.float32),
            jnp.zeros(down_matrix.shape, jnp.float32),
        )
        packed = (
            group_tokens.reshape(chunks, chunk, -1),
            group_cot.reshape(chunks, chunk, -1),
            jnp.transpose(local_weight.reshape(local_experts, chunks, chunk, 1), (1, 0, 2, 3)),
        )
        (gate_grad, up_grad, down_grad), (mixed_parts, input_parts) = lax.scan(
            step, zeros, packed
        )
        mixed_part = mixed_parts.reshape(group_count, -1)
        input_part = input_parts.reshape(group_count, -1)
    gate_grad = gate_grad.astype(jnp.bfloat16)
    up_grad = up_grad.astype(jnp.bfloat16)
    mixed = reduce_scatter(mixed_part).astype(jnp.bfloat16)
    input_grad = reduce_scatter(input_part).astype(jnp.bfloat16)

    peers = [shifted(down_weight, "rep", 1 << bit_index) for bit_index in range(ROUNDS)]
    peer_down = peers[0]
    for bit_index in range(1, ROUNDS):
        peer_down = jnp.where(round_k[0] == bit_index, peers[bit_index], peer_down)
    bias_one = 1.0 - beta_one**step_count
    bias_two = 1.0 - beta_two**step_count
    first = beta_one * moment1[0] + (1.0 - beta_one) * down_grad
    second = beta_two * moment2[0] + (1.0 - beta_two) * down_grad * down_grad
    own_down = down_matrix.astype(jnp.float32)
    averaged = (own_down + peer_down[0].astype(jnp.float32)) * 0.5
    update = first / bias_one / (jnp.sqrt(second / bias_two) + adam_eps)
    new_down = (averaged - learn_rate * (update + decay_rate * own_down)).astype(jnp.bfloat16)
    return (
        mixed,
        input_grad,
        gate_grad[None],
        up_grad[None],
        new_down[None],
        first[None],
        second[None],
    )


def solution(mesh):
    return jax.shard_map(
        per_device,
        mesh=mesh,
        in_specs=(
            P(("rep", "exp"), None),
            P(("rep", "exp"), None),
            P(("rep", "exp"), None),
            P(("rep", "exp"), None),
            P("rep", "exp", None, None),
            P("rep", "exp", None, None),
            P("rep", "exp", None, None),
            P("rep", "exp", None, None),
            P("rep", "exp", None, None),
            P("exp"),
        ),
        out_specs=(
            P(("rep", "exp"), None),
            P(("rep", "exp"), None),
            P("rep", "exp", None, None),
            P("rep", "exp", None, None),
            P("rep", "exp", None, None),
            P("rep", "exp", None, None),
            P("rep", "exp", None, None),
        ),
        check_vma=False,
    )
```

```python
import jax
import jax.numpy as jnp
from jax import lax
from jax.sharding import PartitionSpec as P

ROUNDS = 2
CHUNK_ROWS = 2048
RING_MAX = 8


beta_one = 0.9
beta_two = 0.999
learn_rate = 0.01
decay_rate = 0.1
adam_eps = 1e-08
step_count = 100.0


def shifted(value, axis, by):
    size = lax.axis_size(axis)
    return lax.ppermute(value, axis, [(i, (i + by) % size) for i in range(size)])


def as_bf16(value):
    return lax.reduce_precision(value, exponent_bits=8, mantissa_bits=7)


def dense_weights(expert_ids, combine, experts):
    expert_iota = jnp.arange(experts, dtype=jnp.int32)
    hit = expert_ids[:, :, None] == expert_iota[None, None, :]
    picked = jnp.where(hit, combine.astype(jnp.float32)[:, :, None], 0.0)
    return jnp.sum(picked, axis=1).astype(jnp.bfloat16)


def ring_order(size):
    return list(range(0, size, 2)) + list(range(size - 1 - size % 2, 0, -2))


def ring_pairs(ring, step):
    size = len(ring)
    return [(ring[q], ring[(q + step) % size]) for q in range(size)]


def paired_shift(ahead_value, behind_value, axis, ring):
    if behind_value is None:
        return lax.ppermute(ahead_value, axis, ring_pairs(ring, 1)), None
    if ahead_value is None:
        return None, lax.ppermute(behind_value, axis, ring_pairs(ring, -1))
    ahead_value, behind_value = lax.optimization_barrier((ahead_value, behind_value))
    ahead_value = lax.ppermute(ahead_value, axis, ring_pairs(ring, 1))
    behind_value = lax.ppermute(behind_value, axis, ring_pairs(ring, -1))
    return lax.optimization_barrier((ahead_value, behind_value))


def ring_all_gather(shard, axis, ring):
    size = len(ring)
    ahead = size // 2
    behind = size - 1 - ahead
    got = {0: shard}
    ahead_value = shard
    behind_value = shard
    for step in range(max(ahead, behind)):
        ahead_value, behind_value = paired_shift(
            ahead_value if step < ahead else None,
            behind_value if step < behind else None,
            axis,
            ring,
        )
        if step < ahead:
            got[-(step + 1)] = ahead_value
        if step < behind:
            got[step + 1] = behind_value
    return jnp.concatenate([got[offset] for offset in range(-ahead, behind + 1)])


def ring_reduce_scatter(part, axis, ring, wire_dtype):
    size = len(ring)
    ahead = size // 2
    behind = size - 1 - ahead
    blocks = part.reshape((size, part.shape[0] // size) + part.shape[1:])

    def block_at(offset):
        return blocks[(offset + ahead) % size]

    def to_wire(value):
        return value.astype(wire_dtype)

    result = block_at(0)
    first_ahead, first_behind = lax.optimization_barrier((block_at(ahead), block_at(-behind)))
    ahead_value = to_wire(first_ahead) if ahead else None
    behind_value = to_wire(first_behind) if behind else None
    for step in range(max(ahead, behind)):
        ahead_value, behind_value = paired_shift(
            ahead_value if step < ahead else None,
            behind_value if step < behind else None,
            axis,
            ring,
        )
        if step < ahead - 1:
            ahead_value = to_wire(ahead_value.astype(part.dtype) + block_at(ahead - step - 1))
        elif step == ahead - 1:
            result = result + ahead_value.astype(part.dtype)
        if step < behind - 1:
            behind_value = to_wire(behind_value.astype(part.dtype) + block_at(-behind + step + 1))
        elif step == behind - 1:
            result = result + behind_value.astype(part.dtype)
    return result


def per_device(
    tokens,
    cotangent,
    expert_ids,
    combine,
    gate_weight,
    up_weight,
    down_weight,
    moment1,
    moment2,
    round_k,
):
    local_experts = gate_weight.shape[1]
    devices_exp = lax.axis_size("exp")
    experts = local_experts * devices_exp
    my_exp = lax.axis_index("exp")

    token_count, model_width = tokens.shape
    weight_table = dense_weights(expert_ids, combine, experts)
    weight_rows = -(-(token_count * experts) // model_width)
    weight_rows = -(-weight_rows // 8) * 8
    weight_flat = jnp.pad(
        weight_table.reshape(-1), (0, weight_rows * model_width - token_count * experts)
    )
    packed_tokens = jnp.concatenate([tokens, weight_flat.reshape(weight_rows, model_width)])
    ring = ring_order(devices_exp)
    use_ring = devices_exp <= RING_MAX

    def gather(value):
        if use_ring:
            return ring_all_gather(value, "exp", ring)
        return lax.all_gather(value, "exp", axis=0, tiled=True)

    def reduce_scatter(value):
        if use_ring:
            return ring_reduce_scatter(value, "exp", ring, jnp.bfloat16)
        return lax.psum_scatter(value, "exp", scatter_dimension=0, tiled=True)

    gathered = gather(packed_tokens[None])
    group_tokens = gathered[:, :token_count].reshape(devices_exp * token_count, model_width)
    group_weight = (
        gathered[:, token_count:]
        .reshape(devices_exp, -1)[:, : token_count * experts]
        .reshape(devices_exp * token_count, experts)
    )
    _, cotangent = lax.optimization_barrier((gathered, cotangent))
    group_cot = gather(cotangent)
    local_weight = lax.dynamic_slice_in_dim(
        group_weight, my_exp * local_experts, local_experts, axis=1
    ).astype(jnp.float32)
    local_weight = jnp.transpose(local_weight)[:, :, None]

    gate_matrix = gate_weight[0]
    up_matrix = up_weight[0]
    down_matrix = down_weight[0]

    hidden_width = gate_matrix.shape[2]
    joint_matrix = jnp.concatenate([gate_matrix, up_matrix], axis=2)

    def chunk_pass(chunk_tokens, chunk_cot, chunk_weight):
        gate_value = jnp.einsum(
            "td,edh->eth", chunk_tokens, gate_matrix, preferred_element_type=jnp.float32
        )
        up_value = jnp.einsum(
            "td,edh->eth", chunk_tokens, up_matrix, preferred_element_type=jnp.float32
        )
        sigmoid_gate = jax.nn.sigmoid(gate_value)
        active = gate_value * sigmoid_gate
        hidden = (active * up_value).astype(jnp.bfloat16)
        expert_out = as_bf16(
            jnp.einsum("eth,ehd->etd", hidden, down_matrix, preferred_element_type=jnp.float32)
        )
        mixed_part = jnp.sum(chunk_weight * expert_out, axis=0)
        chunk_cot, mixed_part = lax.optimization_barrier((chunk_cot, mixed_part))
        slot_cot = (chunk_weight * chunk_cot.astype(jnp.float32)[None]).astype(jnp.bfloat16)
        hidden_cot = jnp.einsum(
            "etd,ehd->eth", slot_cot, down_matrix, preferred_element_type=jnp.float32
        )
        gate_cot = (
            hidden_cot * up_value * sigmoid_gate * (1.0 + gate_value * (1.0 - sigmoid_gate))
        ).astype(jnp.bfloat16)
        up_cot = (hidden_cot * active).astype(jnp.bfloat16)
        down_grad = jnp.einsum(
            "eth,etd->ehd", hidden, slot_cot, preferred_element_type=jnp.float32
        )
        joint_cot = jnp.concatenate([gate_cot, up_cot], axis=2)
        joint_grad = jnp.einsum(
            "td,eth->edh", chunk_tokens, joint_cot, preferred_element_type=jnp.float32
        )
        gate_grad = joint_grad[..., :hidden_width]
        up_grad = joint_grad[..., hidden_width:]
        input_cot = as_bf16(
            jnp.einsum("eth,edh->etd", joint_cot, joint_matrix, preferred_element_type=jnp.float32)
        )
        input_part = jnp.sum(input_cot, axis=0)
        return mixed_part, input_part, gate_grad, up_grad, down_grad

    group_count = group_tokens.shape[0]
    chunk = min(group_count, CHUNK_ROWS)
    chunks = group_count // chunk
    if chunks == 1:
        mixed_part, input_part, gate_grad, up_grad, down_grad = chunk_pass(
            group_tokens, group_cot, local_weight
        )
    else:

        def step(carry, packed):
            parts = chunk_pass(*packed)
            grads = tuple(acc + part for acc, part in zip(carry, parts[2:]))
            return grads, parts[:2]

        zeros = (
            jnp.zeros(gate_matrix.shape, jnp.float32),
            jnp.zeros(up_matrix.shape, jnp.float32),
            jnp.zeros(down_matrix.shape, jnp.float32),
        )
        packed = (
            group_tokens.reshape(chunks, chunk, -1),
            group_cot.reshape(chunks, chunk, -1),
            jnp.transpose(local_weight.reshape(local_experts, chunks, chunk, 1), (1, 0, 2, 3)),
        )
        (gate_grad, up_grad, down_grad), (mixed_parts, input_parts) = lax.scan(
            step, zeros, packed
        )
        mixed_part = mixed_parts.reshape(group_count, -1)
        input_part = input_parts.reshape(group_count, -1)
    gate_grad = gate_grad.astype(jnp.bfloat16)
    up_grad = up_grad.astype(jnp.bfloat16)
    mixed = reduce_scatter(mixed_part).astype(jnp.bfloat16)
    input_grad = reduce_scatter(input_part).astype(jnp.bfloat16)

    peers = [shifted(down_weight, "rep", 1 << bit_index) for bit_index in range(ROUNDS)]
    peer_down = peers[0]
    for bit_index in range(1, ROUNDS):
        peer_down = jnp.where(round_k[0] == bit_index, peers[bit_index], peer_down)
    bias_one = 1.0 - beta_one**step_count
    bias_two = 1.0 - beta_two**step_count
    first = beta_one * moment1[0] + (1.0 - beta_one) * down_grad
    second = beta_two * moment2[0] + (1.0 - beta_two) * down_grad * down_grad
    own_down = down_matrix.astype(jnp.float32)
    averaged = (own_down + peer_down[0].astype(jnp.float32)) * 0.5
    update = first / bias_one / (jnp.sqrt(second / bias_two) + adam_eps)
    new_down = (averaged - learn_rate * (update + decay_rate * own_down)).astype(jnp.bfloat16)
    return (
        mixed,
        input_grad,
        gate_grad[None],
        up_grad[None],
        new_down[None],
        first[None],
        second[None],
    )


def solution(mesh):
    return jax.shard_map(
        per_device,
        mesh=mesh,
        in_specs=(
            P(("rep", "exp"), None),
            P(("rep", "exp"), None),
            P(("rep", "exp"), None),
            P(("rep", "exp"), None),
            P("rep", "exp", None, None),
            P("rep", "exp", None, None),
            P("rep", "exp", None, None),
            P("rep", "exp", None, None),
            P("rep", "exp", None, None),
            P("exp"),
        ),
        out_specs=(
            P(("rep", "exp"), None),
            P(("rep", "exp"), None),
            P("rep", "exp", None, None),
            P("rep", "exp", None, None),
            P("rep", "exp", None, None),
            P("rep", "exp", None, None),
            P("rep", "exp", None, None),
        ),
        check_vma=False,
    )
```

```python
import jax
import jax.numpy as jnp
from jax import lax
from jax.sharding import PartitionSpec as P

ROUNDS = 2
CHUNK_ROWS = 2048
RING_MAX = 8


beta_one = 0.9
beta_two = 0.999
learn_rate = 0.01
decay_rate = 0.1
adam_eps = 1e-08
step_count = 100.0


def shifted(value, axis, by):
    size = lax.axis_size(axis)
    return lax.ppermute(value, axis, [(i, (i + by) % size) for i in range(size)])


def as_bf16(value):
    return lax.reduce_precision(value, exponent_bits=8, mantissa_bits=7)


def dense_weights(expert_ids, combine, experts):
    expert_iota = jnp.arange(experts, dtype=jnp.int32)
    hit = expert_ids[:, :, None] == expert_iota[None, None, :]
    picked = jnp.where(hit, combine.astype(jnp.float32)[:, :, None], 0.0)
    return jnp.sum(picked, axis=1).astype(jnp.bfloat16)


def ring_order(size):
    return list(range(0, size, 2)) + list(range(size - 1 - size % 2, 0, -2))


def ring_pairs(ring, step):
    size = len(ring)
    return [(ring[q], ring[(q + step) % size]) for q in range(size)]


def paired_shift(ahead_value, behind_value, axis, ring):
    if behind_value is None:
        return lax.ppermute(ahead_value, axis, ring_pairs(ring, 1)), None
    if ahead_value is None:
        return None, lax.ppermute(behind_value, axis, ring_pairs(ring, -1))
    ahead_value, behind_value = lax.optimization_barrier((ahead_value, behind_value))
    ahead_value = lax.ppermute(ahead_value, axis, ring_pairs(ring, 1))
    behind_value = lax.ppermute(behind_value, axis, ring_pairs(ring, -1))
    return lax.optimization_barrier((ahead_value, behind_value))


def ring_all_gather(shard, axis, ring):
    size = len(ring)
    ahead = size // 2
    behind = size - 1 - ahead
    got = {0: shard}
    ahead_value = shard
    behind_value = shard
    for step in range(max(ahead, behind)):
        ahead_value, behind_value = paired_shift(
            ahead_value if step < ahead else None,
            behind_value if step < behind else None,
            axis,
            ring,
        )
        if step < ahead:
            got[-(step + 1)] = ahead_value
        if step < behind:
            got[step + 1] = behind_value
    return jnp.concatenate([got[offset] for offset in range(-ahead, behind + 1)])


def ring_reduce_scatter(part, axis, ring, wire_dtype):
    size = len(ring)
    ahead = size // 2
    behind = size - 1 - ahead
    blocks = part.reshape((size, part.shape[0] // size) + part.shape[1:])

    def block_at(offset):
        return blocks[(offset + ahead) % size]

    def to_wire(value):
        return value.astype(wire_dtype)

    result = block_at(0)
    first_ahead, first_behind = lax.optimization_barrier((block_at(ahead), block_at(-behind)))
    ahead_value = to_wire(first_ahead) if ahead else None
    behind_value = to_wire(first_behind) if behind else None
    for step in range(max(ahead, behind)):
        ahead_value, behind_value = paired_shift(
            ahead_value if step < ahead else None,
            behind_value if step < behind else None,
            axis,
            ring,
        )
        if step < ahead - 1:
            ahead_value = to_wire(ahead_value.astype(part.dtype) + block_at(ahead - step - 1))
        elif step == ahead - 1:
            result = result + ahead_value.astype(part.dtype)
        if step < behind - 1:
            behind_value = to_wire(behind_value.astype(part.dtype) + block_at(-behind + step + 1))
        elif step == behind - 1:
            result = result + behind_value.astype(part.dtype)
    return result


def per_device(
    tokens,
    cotangent,
    expert_ids,
    combine,
    gate_weight,
    up_weight,
    down_weight,
    moment1,
    moment2,
    round_k,
):
    local_experts = gate_weight.shape[1]
    devices_exp = lax.axis_size("exp")
    experts = local_experts * devices_exp
    my_exp = lax.axis_index("exp")

    token_count, model_width = tokens.shape
    weight_table = dense_weights(expert_ids, combine, experts)
    weight_rows = -(-(token_count * experts) // model_width)
    weight_rows = -(-weight_rows // 8) * 8
    weight_flat = jnp.pad(
        weight_table.reshape(-1), (0, weight_rows * model_width - token_count * experts)
    )
    packed_tokens = jnp.concatenate([tokens, weight_flat.reshape(weight_rows, model_width)])
    ring = ring_order(devices_exp)
    use_ring = devices_exp <= RING_MAX

    def gather(value):
        if use_ring:
            return ring_all_gather(value, "exp", ring)
        return lax.all_gather(value, "exp", axis=0, tiled=True)

    def reduce_scatter(value):
        if use_ring:
            return ring_reduce_scatter(value, "exp", ring, jnp.bfloat16)
        return lax.psum_scatter(value, "exp", scatter_dimension=0, tiled=True)

    gathered = gather(packed_tokens[None])
    group_tokens = gathered[:, :token_count].reshape(devices_exp * token_count, model_width)
    group_weight = (
        gathered[:, token_count:]
        .reshape(devices_exp, -1)[:, : token_count * experts]
        .reshape(devices_exp * token_count, experts)
    )
    _, cotangent = lax.optimization_barrier((gathered, cotangent))
    group_cot = gather(cotangent)
    local_weight = lax.dynamic_slice_in_dim(
        group_weight, my_exp * local_experts, local_experts, axis=1
    ).astype(jnp.float32)
    local_weight = jnp.transpose(local_weight)[:, :, None]

    gate_matrix = gate_weight[0]
    up_matrix = up_weight[0]
    down_matrix = down_weight[0]

    hidden_width = gate_matrix.shape[2]
    joint_matrix = jnp.concatenate([gate_matrix, up_matrix], axis=2)

    def chunk_pass(chunk_tokens, chunk_cot, chunk_weight):
        gate_value = jnp.einsum(
            "td,edh->eth", chunk_tokens, gate_matrix, preferred_element_type=jnp.float32
        )
        up_value = jnp.einsum(
            "td,edh->eth", chunk_tokens, up_matrix, preferred_element_type=jnp.float32
        )
        sigmoid_gate = jax.nn.sigmoid(gate_value)
        active = gate_value * sigmoid_gate
        hidden = (active * up_value).astype(jnp.bfloat16)
        expert_out = as_bf16(
            jnp.einsum("eth,ehd->etd", hidden, down_matrix, preferred_element_type=jnp.float32)
        )
        mixed_part = jnp.sum(chunk_weight * expert_out, axis=0)
        chunk_cot, mixed_part = lax.optimization_barrier((chunk_cot, mixed_part))
        slot_cot = chunk_weight.astype(jnp.bfloat16) * chunk_cot[None]
        hidden_cot = jnp.einsum(
            "etd,ehd->eth", slot_cot, down_matrix, preferred_element_type=jnp.float32
        )
        gate_cot = (
            hidden_cot * up_value * sigmoid_gate * (1.0 + gate_value * (1.0 - sigmoid_gate))
        ).astype(jnp.bfloat16)
        up_cot = (hidden_cot * active).astype(jnp.bfloat16)
        down_grad = jnp.einsum(
            "eth,etd->ehd", hidden, slot_cot, preferred_element_type=jnp.float32
        )
        joint_cot = jnp.concatenate([gate_cot, up_cot], axis=2)
        joint_grad = jnp.einsum(
            "td,eth->edh", chunk_tokens, joint_cot, preferred_element_type=jnp.float32
        )
        gate_grad = joint_grad[..., :hidden_width]
        up_grad = joint_grad[..., hidden_width:]
        input_cot = as_bf16(
            jnp.einsum("eth,edh->etd", joint_cot, joint_matrix, preferred_element_type=jnp.float32)
        )
        input_part = jnp.sum(input_cot, axis=0)
        return mixed_part, input_part, gate_grad, up_grad, down_grad

    group_count = group_tokens.shape[0]
    chunk = min(group_count, CHUNK_ROWS)
    chunks = group_count // chunk
    if chunks == 1:
        mixed_part, input_part, gate_grad, up_grad, down_grad = chunk_pass(
            group_tokens, group_cot, local_weight
        )
    else:

        def step(carry, packed):
            parts = chunk_pass(*packed)
            grads = tuple(acc + part for acc, part in zip(carry, parts[2:]))
            return grads, parts[:2]

        zeros = (
            jnp.zeros(gate_matrix.shape, jnp.float32),
            jnp.zeros(up_matrix.shape, jnp.float32),
            jnp.zeros(down_matrix.shape, jnp.float32),
        )
        packed = (
            group_tokens.reshape(chunks, chunk, -1),
            group_cot.reshape(chunks, chunk, -1),
            jnp.transpose(local_weight.reshape(local_experts, chunks, chunk, 1), (1, 0, 2, 3)),
        )
        (gate_grad, up_grad, down_grad), (mixed_parts, input_parts) = lax.scan(
            step, zeros, packed
        )
        mixed_part = mixed_parts.reshape(group_count, -1)
        input_part = input_parts.reshape(group_count, -1)
    gate_grad = gate_grad.astype(jnp.bfloat16)
    up_grad = up_grad.astype(jnp.bfloat16)
    mixed = reduce_scatter(mixed_part).astype(jnp.bfloat16)
    input_grad = reduce_scatter(input_part).astype(jnp.bfloat16)

    peers = [shifted(down_weight, "rep", 1 << bit_index) for bit_index in range(ROUNDS)]
    peer_down = peers[0]
    for bit_index in range(1, ROUNDS):
        peer_down = jnp.where(round_k[0] == bit_index, peers[bit_index], peer_down)
    bias_one = 1.0 - beta_one**step_count
    bias_two = 1.0 - beta_two**step_count
    first = beta_one * moment1[0] + (1.0 - beta_one) * down_grad
    second = beta_two * moment2[0] + (1.0 - beta_two) * down_grad * down_grad
    own_down = down_matrix.astype(jnp.float32)
    averaged = (own_down + peer_down[0].astype(jnp.float32)) * 0.5
    update = first / bias_one / (jnp.sqrt(second / bias_two) + adam_eps)
    new_down = (averaged - learn_rate * (update + decay_rate * own_down)).astype(jnp.bfloat16)
    return (
        mixed,
        input_grad,
        gate_grad[None],
        up_grad[None],
        new_down[None],
        first[None],
        second[None],
    )


def solution(mesh):
    return jax.shard_map(
        per_device,
        mesh=mesh,
        in_specs=(
            P(("rep", "exp"), None),
            P(("rep", "exp"), None),
            P(("rep", "exp"), None),
            P(("rep", "exp"), None),
            P("rep", "exp", None, None),
            P("rep", "exp", None, None),
            P("rep", "exp", None, None),
            P("rep", "exp", None, None),
            P("rep", "exp", None, None),
            P("exp"),
        ),
        out_specs=(
            P(("rep", "exp"), None),
            P(("rep", "exp"), None),
            P("rep", "exp", None, None),
            P("rep", "exp", None, None),
            P("rep", "exp", None, None),
            P("rep", "exp", None, None),
            P("rep", "exp", None, None),
        ),
        check_vma=False,
    )
```

```python
import jax
import jax.numpy as jnp
from jax import lax
from jax.sharding import PartitionSpec as P

ROUNDS = 2
CHUNK_ROWS = 2048
RING_MAX = 8


beta_one = 0.9
beta_two = 0.999
learn_rate = 0.01
decay_rate = 0.1
adam_eps = 1e-08
step_count = 100.0


def shifted(value, axis, by):
    size = lax.axis_size(axis)
    return lax.ppermute(value, axis, [(i, (i + by) % size) for i in range(size)])


def as_bf16(value):
    return lax.reduce_precision(value, exponent_bits=8, mantissa_bits=7)


def dense_weights(expert_ids, combine, experts):
    expert_iota = jnp.arange(experts, dtype=jnp.int32)
    hit = expert_ids[:, :, None] == expert_iota[None, None, :]
    picked = jnp.where(hit, combine.astype(jnp.float32)[:, :, None], 0.0)
    return jnp.sum(picked, axis=1).astype(jnp.bfloat16)


def ring_order(size):
    return list(range(0, size, 2)) + list(range(size - 1 - size % 2, 0, -2))


def ring_pairs(ring, step):
    size = len(ring)
    return [(ring[q], ring[(q + step) % size]) for q in range(size)]


def paired_shift(ahead_value, behind_value, axis, ring):
    if behind_value is None:
        return lax.ppermute(ahead_value, axis, ring_pairs(ring, 1)), None
    if ahead_value is None:
        return None, lax.ppermute(behind_value, axis, ring_pairs(ring, -1))
    ahead_value, behind_value = lax.optimization_barrier((ahead_value, behind_value))
    ahead_value = lax.ppermute(ahead_value, axis, ring_pairs(ring, 1))
    behind_value = lax.ppermute(behind_value, axis, ring_pairs(ring, -1))
    return lax.optimization_barrier((ahead_value, behind_value))


def ring_all_gather(shard, axis, ring):
    size = len(ring)
    ahead = size // 2
    behind = size - 1 - ahead
    got = {0: shard}
    ahead_value = shard
    behind_value = shard
    for step in range(max(ahead, behind)):
        ahead_value, behind_value = paired_shift(
            ahead_value if step < ahead else None,
            behind_value if step < behind else None,
            axis,
            ring,
        )
        if step < ahead:
            got[-(step + 1)] = ahead_value
        if step < behind:
            got[step + 1] = behind_value
    return jnp.concatenate([got[offset] for offset in range(-ahead, behind + 1)])


def ring_reduce_scatter(part, axis, ring, wire_dtype):
    size = len(ring)
    ahead = size // 2
    behind = size - 1 - ahead
    blocks = part.reshape((size, part.shape[0] // size) + part.shape[1:])

    def block_at(offset):
        return blocks[(offset + ahead) % size]

    def to_wire(value):
        return value.astype(wire_dtype)

    result = block_at(0)
    first_ahead, first_behind = lax.optimization_barrier((block_at(ahead), block_at(-behind)))
    ahead_value = to_wire(first_ahead) if ahead else None
    behind_value = to_wire(first_behind) if behind else None
    for step in range(max(ahead, behind)):
        ahead_value, behind_value = paired_shift(
            ahead_value if step < ahead else None,
            behind_value if step < behind else None,
            axis,
            ring,
        )
        if step < ahead - 1:
            ahead_value = to_wire(ahead_value.astype(part.dtype) + block_at(ahead - step - 1))
        elif step == ahead - 1:
            result = result + ahead_value.astype(part.dtype)
        if step < behind - 1:
            behind_value = to_wire(behind_value.astype(part.dtype) + block_at(-behind + step + 1))
        elif step == behind - 1:
            result = result + behind_value.astype(part.dtype)
    return result


def per_device(
    tokens,
    cotangent,
    expert_ids,
    combine,
    gate_weight,
    up_weight,
    down_weight,
    moment1,
    moment2,
    round_k,
):
    local_experts = gate_weight.shape[1]
    devices_exp = lax.axis_size("exp")
    experts = local_experts * devices_exp
    my_exp = lax.axis_index("exp")

    token_count, model_width = tokens.shape
    weight_table = dense_weights(expert_ids, combine, experts)
    weight_rows = -(-(token_count * experts) // model_width)
    weight_rows = -(-weight_rows // 8) * 8
    weight_flat = jnp.pad(
        weight_table.reshape(-1), (0, weight_rows * model_width - token_count * experts)
    )
    packed_cot = jnp.concatenate([cotangent, weight_flat.reshape(weight_rows, model_width)])
    ring = ring_order(devices_exp)
    use_ring = devices_exp <= RING_MAX

    def gather(value):
        if use_ring:
            return ring_all_gather(value, "exp", ring)
        return lax.all_gather(value, "exp", axis=0, tiled=True)

    def reduce_scatter(value):
        if use_ring:
            return ring_reduce_scatter(value, "exp", ring, jnp.bfloat16)
        return lax.psum_scatter(value, "exp", scatter_dimension=0, tiled=True)

    group_tokens = gather(tokens)
    _, packed_cot = lax.optimization_barrier((group_tokens, packed_cot))
    gathered = gather(packed_cot[None])
    group_cot = gathered[:, :token_count].reshape(devices_exp * token_count, model_width)
    group_weight = (
        gathered[:, token_count:]
        .reshape(devices_exp, -1)[:, : token_count * experts]
        .reshape(devices_exp * token_count, experts)
    )
    local_weight = lax.dynamic_slice_in_dim(
        group_weight, my_exp * local_experts, local_experts, axis=1
    ).astype(jnp.float32)
    local_weight = jnp.transpose(local_weight)[:, :, None]

    gate_matrix = gate_weight[0]
    up_matrix = up_weight[0]
    down_matrix = down_weight[0]

    hidden_width = gate_matrix.shape[2]
    joint_matrix = jnp.concatenate([gate_matrix, up_matrix], axis=2)

    def chunk_pass(chunk_tokens, chunk_cot, chunk_weight):
        gate_value = jnp.einsum(
            "td,edh->eth", chunk_tokens, gate_matrix, preferred_element_type=jnp.float32
        )
        up_value = jnp.einsum(
            "td,edh->eth", chunk_tokens, up_matrix, preferred_element_type=jnp.float32
        )
        sigmoid_gate = jax.nn.sigmoid(gate_value)
        active = gate_value * sigmoid_gate
        hidden = (active * up_value).astype(jnp.bfloat16)
        expert_out = as_bf16(
            jnp.einsum("eth,ehd->etd", hidden, down_matrix, preferred_element_type=jnp.float32)
        )
        mixed_part = jnp.sum(chunk_weight * expert_out, axis=0)
        chunk_cot, mixed_part = lax.optimization_barrier((chunk_cot, mixed_part))
        slot_cot = chunk_weight.astype(jnp.bfloat16) * chunk_cot[None]
        hidden_cot = jnp.einsum(
            "etd,ehd->eth", slot_cot, down_matrix, preferred_element_type=jnp.float32
        )
        gate_cot = (
            hidden_cot * up_value * sigmoid_gate * (1.0 + gate_value * (1.0 - sigmoid_gate))
        ).astype(jnp.bfloat16)
        up_cot = (hidden_cot * active).astype(jnp.bfloat16)
        down_grad = jnp.einsum(
            "eth,etd->ehd", hidden, slot_cot, preferred_element_type=jnp.float32
        )
        joint_cot = jnp.concatenate([gate_cot, up_cot], axis=2)
        joint_grad = jnp.einsum(
            "td,eth->edh", chunk_tokens, joint_cot, preferred_element_type=jnp.float32
        )
        gate_grad = joint_grad[..., :hidden_width]
        up_grad = joint_grad[..., hidden_width:]
        input_cot = as_bf16(
            jnp.einsum("eth,edh->etd", joint_cot, joint_matrix, preferred_element_type=jnp.float32)
        )
        input_part = jnp.sum(input_cot, axis=0)
        return mixed_part, input_part, gate_grad, up_grad, down_grad

    group_count = group_tokens.shape[0]
    chunk = min(group_count, CHUNK_ROWS)
    chunks = group_count // chunk
    if chunks == 1:
        mixed_part, input_part, gate_grad, up_grad, down_grad = chunk_pass(
            group_tokens, group_cot, local_weight
        )
    else:

        def step(carry, packed):
            parts = chunk_pass(*packed)
            grads = tuple(acc + part for acc, part in zip(carry, parts[2:]))
            return grads, parts[:2]

        zeros = (
            jnp.zeros(gate_matrix.shape, jnp.float32),
            jnp.zeros(up_matrix.shape, jnp.float32),
            jnp.zeros(down_matrix.shape, jnp.float32),
        )
        packed = (
            group_tokens.reshape(chunks, chunk, -1),
            group_cot.reshape(chunks, chunk, -1),
            jnp.transpose(local_weight.reshape(local_experts, chunks, chunk, 1), (1, 0, 2, 3)),
        )
        (gate_grad, up_grad, down_grad), (mixed_parts, input_parts) = lax.scan(
            step, zeros, packed
        )
        mixed_part = mixed_parts.reshape(group_count, -1)
        input_part = input_parts.reshape(group_count, -1)
    gate_grad = gate_grad.astype(jnp.bfloat16)
    up_grad = up_grad.astype(jnp.bfloat16)
    mixed = reduce_scatter(mixed_part).astype(jnp.bfloat16)
    input_grad = reduce_scatter(input_part).astype(jnp.bfloat16)

    peers = [shifted(down_weight, "rep", 1 << bit_index) for bit_index in range(ROUNDS)]
    peer_down = peers[0]
    for bit_index in range(1, ROUNDS):
        peer_down = jnp.where(round_k[0] == bit_index, peers[bit_index], peer_down)
    bias_one = 1.0 - beta_one**step_count
    bias_two = 1.0 - beta_two**step_count
    first = beta_one * moment1[0] + (1.0 - beta_one) * down_grad
    second = beta_two * moment2[0] + (1.0 - beta_two) * down_grad * down_grad
    own_down = down_matrix.astype(jnp.float32)
    averaged = (own_down + peer_down[0].astype(jnp.float32)) * 0.5
    update = first / bias_one / (jnp.sqrt(second / bias_two) + adam_eps)
    new_down = (averaged - learn_rate * (update + decay_rate * own_down)).astype(jnp.bfloat16)
    return (
        mixed,
        input_grad,
        gate_grad[None],
        up_grad[None],
        new_down[None],
        first[None],
        second[None],
    )


def solution(mesh):
    return jax.shard_map(
        per_device,
        mesh=mesh,
        in_specs=(
            P(("rep", "exp"), None),
            P(("rep", "exp"), None),
            P(("rep", "exp"), None),
            P(("rep", "exp"), None),
            P("rep", "exp", None, None),
            P("rep", "exp", None, None),
            P("rep", "exp", None, None),
            P("rep", "exp", None, None),
            P("rep", "exp", None, None),
            P("exp"),
        ),
        out_specs=(
            P(("rep", "exp"), None),
            P(("rep", "exp"), None),
            P("rep", "exp", None, None),
            P("rep", "exp", None, None),
            P("rep", "exp", None, None),
            P("rep", "exp", None, None),
            P("rep", "exp", None, None),
        ),
        check_vma=False,
    )
```

```python
import jax
import jax.numpy as jnp
from jax import lax
from jax.sharding import PartitionSpec as P

ROUNDS = 2
CHUNK_ROWS = 2048
RING_MAX = 8


beta_one = 0.9
beta_two = 0.999
learn_rate = 0.01
decay_rate = 0.1
adam_eps = 1e-08
step_count = 100.0


def shifted(value, axis, by):
    size = lax.axis_size(axis)
    return lax.ppermute(value, axis, [(i, (i + by) % size) for i in range(size)])


def as_bf16(value):
    return lax.reduce_precision(value, exponent_bits=8, mantissa_bits=7)


def dense_weights(expert_ids, combine, experts):
    expert_iota = jnp.arange(experts, dtype=jnp.int32)
    hit = expert_ids[:, :, None] == expert_iota[None, None, :]
    picked = jnp.where(hit, combine.astype(jnp.float32)[:, :, None], 0.0)
    return jnp.sum(picked, axis=1).astype(jnp.bfloat16)


def ring_order(size):
    return list(range(0, size, 2)) + list(range(size - 1 - size % 2, 0, -2))


def ring_pairs(ring, step):
    size = len(ring)
    return [(ring[q], ring[(q + step) % size]) for q in range(size)]


def paired_shift(ahead_value, behind_value, axis, ring):
    if behind_value is None:
        return lax.ppermute(ahead_value, axis, ring_pairs(ring, 1)), None
    if ahead_value is None:
        return None, lax.ppermute(behind_value, axis, ring_pairs(ring, -1))
    ahead_value, behind_value = lax.optimization_barrier((ahead_value, behind_value))
    ahead_value = lax.ppermute(ahead_value, axis, ring_pairs(ring, 1))
    behind_value = lax.ppermute(behind_value, axis, ring_pairs(ring, -1))
    return lax.optimization_barrier((ahead_value, behind_value))


def ring_all_gather(shard, axis, ring):
    size = len(ring)
    ahead = size // 2
    behind = size - 1 - ahead
    got = {0: shard}
    ahead_value = shard
    behind_value = shard
    for step in range(max(ahead, behind)):
        ahead_value, behind_value = paired_shift(
            ahead_value if step < ahead else None,
            behind_value if step < behind else None,
            axis,
            ring,
        )
        if step < ahead:
            got[-(step + 1)] = ahead_value
        if step < behind:
            got[step + 1] = behind_value
    return jnp.concatenate([got[offset] for offset in range(-ahead, behind + 1)])


def ring_reduce_scatter(part, axis, ring, wire_dtype):
    size = len(ring)
    ahead = size // 2
    behind = size - 1 - ahead
    blocks = part.reshape((size, part.shape[0] // size) + part.shape[1:])

    def block_at(offset):
        return blocks[(offset + ahead) % size]

    def to_wire(value):
        return value.astype(wire_dtype)

    result = block_at(0)
    first_ahead, first_behind = lax.optimization_barrier((block_at(ahead), block_at(-behind)))
    ahead_value = to_wire(first_ahead) if ahead else None
    behind_value = to_wire(first_behind) if behind else None
    for step in range(max(ahead, behind)):
        ahead_value, behind_value = paired_shift(
            ahead_value if step < ahead else None,
            behind_value if step < behind else None,
            axis,
            ring,
        )
        if step < ahead - 1:
            ahead_value = to_wire(ahead_value.astype(part.dtype) + block_at(ahead - step - 1))
        elif step == ahead - 1:
            result = result + ahead_value.astype(part.dtype)
        if step < behind - 1:
            behind_value = to_wire(behind_value.astype(part.dtype) + block_at(-behind + step + 1))
        elif step == behind - 1:
            result = result + behind_value.astype(part.dtype)
    return result


def per_device(
    tokens,
    cotangent,
    expert_ids,
    combine,
    gate_weight,
    up_weight,
    down_weight,
    moment1,
    moment2,
    round_k,
):
    local_experts = gate_weight.shape[1]
    devices_exp = lax.axis_size("exp")
    experts = local_experts * devices_exp
    my_exp = lax.axis_index("exp")

    token_count, model_width = tokens.shape
    weight_table = dense_weights(expert_ids, combine, experts)
    weight_rows = -(-(token_count * experts) // model_width)
    weight_rows = -(-weight_rows // 8) * 8
    weight_flat = jnp.pad(
        weight_table.reshape(-1), (0, weight_rows * model_width - token_count * experts)
    )
    packed_tokens = jnp.concatenate([tokens, weight_flat.reshape(weight_rows, model_width)])
    ring = ring_order(devices_exp)
    use_ring = devices_exp <= RING_MAX

    def gather(value):
        if use_ring:
            return ring_all_gather(value, "exp", ring)
        return lax.all_gather(value, "exp", axis=0, tiled=True)

    def reduce_scatter(value):
        if use_ring:
            return ring_reduce_scatter(value, "exp", ring, jnp.bfloat16)
        return lax.psum_scatter(value, "exp", scatter_dimension=0, tiled=True)

    gathered = gather(packed_tokens[None])
    group_tokens = gathered[:, :token_count].reshape(devices_exp * token_count, model_width)
    group_weight = (
        gathered[:, token_count:]
        .reshape(devices_exp, -1)[:, : token_count * experts]
        .reshape(devices_exp * token_count, experts)
    )
    _, cotangent = lax.optimization_barrier((gathered, cotangent))
    group_cot = gather(cotangent)
    local_weight = lax.dynamic_slice_in_dim(
        group_weight, my_exp * local_experts, local_experts, axis=1
    ).astype(jnp.float32)
    local_weight = jnp.transpose(local_weight)[:, :, None]

    gate_matrix = gate_weight[0]
    up_matrix = up_weight[0]
    down_matrix = down_weight[0]

    hidden_width = gate_matrix.shape[2]
    joint_matrix = jnp.concatenate([gate_matrix, up_matrix], axis=2)

    def chunk_pass(chunk_tokens, chunk_cot, chunk_weight):
        gate_value = jnp.einsum(
            "td,edh->eth", chunk_tokens, gate_matrix, preferred_element_type=jnp.float32
        )
        up_value = jnp.einsum(
            "td,edh->eth", chunk_tokens, up_matrix, preferred_element_type=jnp.float32
        )
        sigmoid_gate = jax.nn.sigmoid(gate_value)
        active = gate_value * sigmoid_gate
        hidden = (active * up_value).astype(jnp.bfloat16)
        expert_out = as_bf16(
            jnp.einsum("eth,ehd->etd", hidden, down_matrix, preferred_element_type=jnp.float32)
        )
        mixed_part = jnp.sum(chunk_weight * expert_out, axis=0)
        chunk_cot, mixed_part = lax.optimization_barrier((chunk_cot, mixed_part))
        slot_cot = chunk_weight.astype(jnp.bfloat16) * chunk_cot[None]
        hidden_cot = jnp.einsum(
            "etd,ehd->eth", slot_cot, down_matrix, preferred_element_type=jnp.float32
        )
        gate_cot = (
            hidden_cot * up_value * sigmoid_gate * (1.0 + gate_value * (1.0 - sigmoid_gate))
        ).astype(jnp.bfloat16)
        up_cot = (hidden_cot * active).astype(jnp.bfloat16)
        down_grad = jnp.einsum(
            "eth,etd->ehd", hidden, slot_cot, preferred_element_type=jnp.float32
        )
        joint_cot = jnp.concatenate([gate_cot, up_cot], axis=2)
        joint_grad = jnp.einsum(
            "td,eth->edh", chunk_tokens, joint_cot, preferred_element_type=jnp.float32
        )
        gate_grad = joint_grad[..., :hidden_width]
        up_grad = joint_grad[..., hidden_width:]
        input_cot = as_bf16(
            jnp.einsum("eth,edh->etd", joint_cot, joint_matrix, preferred_element_type=jnp.float32)
        )
        input_part = jnp.sum(input_cot, axis=0)
        return mixed_part, input_part, gate_grad, up_grad, down_grad

    group_count = group_tokens.shape[0]
    chunk = min(group_count, CHUNK_ROWS)
    chunks = group_count // chunk
    if chunks == 1:
        mixed_part, input_part, gate_grad, up_grad, down_grad = chunk_pass(
            group_tokens, group_cot, local_weight
        )
    else:

        def step(carry, packed):
            parts = chunk_pass(*packed)
            grads = tuple(acc + part for acc, part in zip(carry, parts[2:]))
            return grads, parts[:2]

        zeros = (
            jnp.zeros(gate_matrix.shape, jnp.float32),
            jnp.zeros(up_matrix.shape, jnp.float32),
            jnp.zeros(down_matrix.shape, jnp.float32),
        )
        packed = (
            group_tokens.reshape(chunks, chunk, -1),
            group_cot.reshape(chunks, chunk, -1),
            jnp.transpose(local_weight.reshape(local_experts, chunks, chunk, 1), (1, 0, 2, 3)),
        )
        (gate_grad, up_grad, down_grad), (mixed_parts, input_parts) = lax.scan(
            step, zeros, packed
        )
        mixed_part = mixed_parts.reshape(group_count, -1)
        input_part = input_parts.reshape(group_count, -1)
    gate_grad = gate_grad.astype(jnp.bfloat16)
    up_grad = up_grad.astype(jnp.bfloat16)
    mixed = reduce_scatter(mixed_part).astype(jnp.bfloat16)
    input_grad = reduce_scatter(input_part).astype(jnp.bfloat16)

    down_send, _ = lax.optimization_barrier((down_weight, group_cot))
    peers = [shifted(down_send, "rep", 1 << bit_index) for bit_index in range(ROUNDS)]
    peer_down = peers[0]
    for bit_index in range(1, ROUNDS):
        peer_down = jnp.where(round_k[0] == bit_index, peers[bit_index], peer_down)
    bias_one = 1.0 - beta_one**step_count
    bias_two = 1.0 - beta_two**step_count
    first = beta_one * moment1[0] + (1.0 - beta_one) * down_grad
    second = beta_two * moment2[0] + (1.0 - beta_two) * down_grad * down_grad
    own_down = down_matrix.astype(jnp.float32)
    averaged = (own_down + peer_down[0].astype(jnp.float32)) * 0.5
    update = first / bias_one / (jnp.sqrt(second / bias_two) + adam_eps)
    new_down = (averaged - learn_rate * (update + decay_rate * own_down)).astype(jnp.bfloat16)
    return (
        mixed,
        input_grad,
        gate_grad[None],
        up_grad[None],
        new_down[None],
        first[None],
        second[None],
    )


def solution(mesh):
    return jax.shard_map(
        per_device,
        mesh=mesh,
        in_specs=(
            P(("rep", "exp"), None),
            P(("rep", "exp"), None),
            P(("rep", "exp"), None),
            P(("rep", "exp"), None),
            P("rep", "exp", None, None),
            P("rep", "exp", None, None),
            P("rep", "exp", None, None),
            P("rep", "exp", None, None),
            P("rep", "exp", None, None),
            P("exp"),
        ),
        out_specs=(
            P(("rep", "exp"), None),
            P(("rep", "exp"), None),
            P("rep", "exp", None, None),
            P("rep", "exp", None, None),
            P("rep", "exp", None, None),
            P("rep", "exp", None, None),
            P("rep", "exp", None, None),
        ),
        check_vma=False,
    )
```

```python
import jax
import jax.numpy as jnp
from jax import lax
from jax.sharding import PartitionSpec as P

ROUNDS = 2
CHUNK_ROWS = 2048
RING_MAX = 8


beta_one = 0.9
beta_two = 0.999
learn_rate = 0.01
decay_rate = 0.1
adam_eps = 1e-08
step_count = 100.0


def shifted(value, axis, by):
    size = lax.axis_size(axis)
    return lax.ppermute(value, axis, [(i, (i + by) % size) for i in range(size)])


def as_bf16(value):
    return lax.reduce_precision(value, exponent_bits=8, mantissa_bits=7)


def dense_weights(expert_ids, combine, experts):
    expert_iota = jnp.arange(experts, dtype=jnp.int32)
    hit = expert_ids[:, :, None] == expert_iota[None, None, :]
    picked = jnp.where(hit, combine.astype(jnp.float32)[:, :, None], 0.0)
    return jnp.sum(picked, axis=1).astype(jnp.bfloat16)


def ring_order(size):
    return list(range(0, size, 2)) + list(range(size - 1 - size % 2, 0, -2))


def ring_pairs(ring, step):
    size = len(ring)
    return [(ring[q], ring[(q + step) % size]) for q in range(size)]


def paired_shift(ahead_value, behind_value, axis, ring):
    if behind_value is None:
        return lax.ppermute(ahead_value, axis, ring_pairs(ring, 1)), None
    if ahead_value is None:
        return None, lax.ppermute(behind_value, axis, ring_pairs(ring, -1))
    ahead_value, behind_value = lax.optimization_barrier((ahead_value, behind_value))
    ahead_value = lax.ppermute(ahead_value, axis, ring_pairs(ring, 1))
    behind_value = lax.ppermute(behind_value, axis, ring_pairs(ring, -1))
    return lax.optimization_barrier((ahead_value, behind_value))


def ring_all_gather(shard, axis, ring):
    size = len(ring)
    ahead = size // 2
    behind = size - 1 - ahead
    got = {0: shard}
    ahead_value = shard
    behind_value = shard
    for step in range(max(ahead, behind)):
        ahead_value, behind_value = paired_shift(
            ahead_value if step < ahead else None,
            behind_value if step < behind else None,
            axis,
            ring,
        )
        if step < ahead:
            got[-(step + 1)] = ahead_value
        if step < behind:
            got[step + 1] = behind_value
    return jnp.concatenate([got[offset] for offset in range(-ahead, behind + 1)])


def ring_reduce_scatter(part, axis, ring, wire_dtype):
    size = len(ring)
    ahead = size // 2
    behind = size - 1 - ahead
    blocks = part.reshape((size, part.shape[0] // size) + part.shape[1:])

    def block_at(offset):
        return blocks[(offset + ahead) % size]

    def to_wire(value):
        return value.astype(wire_dtype)

    result = block_at(0)
    first_ahead, first_behind = lax.optimization_barrier((block_at(ahead), block_at(-behind)))
    ahead_value = to_wire(first_ahead) if ahead else None
    behind_value = to_wire(first_behind) if behind else None
    for step in range(max(ahead, behind)):
        ahead_value, behind_value = paired_shift(
            ahead_value if step < ahead else None,
            behind_value if step < behind else None,
            axis,
            ring,
        )
        if step < ahead - 1:
            ahead_value = to_wire(ahead_value.astype(part.dtype) + block_at(ahead - step - 1))
        elif step == ahead - 1:
            result = result + ahead_value.astype(part.dtype)
        if step < behind - 1:
            behind_value = to_wire(behind_value.astype(part.dtype) + block_at(-behind + step + 1))
        elif step == behind - 1:
            result = result + behind_value.astype(part.dtype)
    return result


def per_device(
    tokens,
    cotangent,
    expert_ids,
    combine,
    gate_weight,
    up_weight,
    down_weight,
    moment1,
    moment2,
    round_k,
):
    local_experts = gate_weight.shape[1]
    devices_exp = lax.axis_size("exp")
    experts = local_experts * devices_exp
    my_exp = lax.axis_index("exp")

    token_count, model_width = tokens.shape
    weight_table = dense_weights(expert_ids, combine, experts)
    weight_rows = -(-(token_count * experts) // model_width)
    weight_rows = -(-weight_rows // 8) * 8
    weight_flat = jnp.pad(
        weight_table.reshape(-1), (0, weight_rows * model_width - token_count * experts)
    )
    packed_tokens = jnp.concatenate([tokens, weight_flat.reshape(weight_rows, model_width)])
    ring = ring_order(devices_exp)
    use_ring = devices_exp <= RING_MAX

    def gather(value):
        if use_ring:
            return ring_all_gather(value, "exp", ring)
        return lax.all_gather(value, "exp", axis=0, tiled=True)

    def reduce_scatter(value):
        if use_ring:
            return ring_reduce_scatter(value, "exp", ring, jnp.bfloat16)
        return lax.psum_scatter(value, "exp", scatter_dimension=0, tiled=True)

    gathered = gather(packed_tokens[None])
    group_tokens = gathered[:, :token_count].reshape(devices_exp * token_count, model_width)
    group_weight = (
        gathered[:, token_count:]
        .reshape(devices_exp, -1)[:, : token_count * experts]
        .reshape(devices_exp * token_count, experts)
    )
    group_cot = gather(cotangent)
    local_weight = lax.dynamic_slice_in_dim(
        group_weight, my_exp * local_experts, local_experts, axis=1
    ).astype(jnp.float32)
    local_weight = jnp.transpose(local_weight)[:, :, None]

    gate_matrix = gate_weight[0]
    up_matrix = up_weight[0]
    down_matrix = down_weight[0]

    hidden_width = gate_matrix.shape[2]
    joint_matrix = jnp.concatenate([gate_matrix, up_matrix], axis=2)

    def chunk_pass(chunk_tokens, chunk_cot, chunk_weight):
        gate_value = jnp.einsum(
            "td,edh->eth", chunk_tokens, gate_matrix, preferred_element_type=jnp.float32
        )
        up_value = jnp.einsum(
            "td,edh->eth", chunk_tokens, up_matrix, preferred_element_type=jnp.float32
        )
        sigmoid_gate = jax.nn.sigmoid(gate_value)
        active = gate_value * sigmoid_gate
        hidden = (active * up_value).astype(jnp.bfloat16)
        expert_out = as_bf16(
            jnp.einsum("eth,ehd->etd", hidden, down_matrix, preferred_element_type=jnp.float32)
        )
        mixed_part = jnp.sum(chunk_weight * expert_out, axis=0)
        chunk_cot, mixed_part = lax.optimization_barrier((chunk_cot, mixed_part))
        slot_cot = chunk_weight.astype(jnp.bfloat16) * chunk_cot[None]
        hidden_cot = jnp.einsum(
            "etd,ehd->eth", slot_cot, down_matrix, preferred_element_type=jnp.float32
        )
        gate_cot = (
            hidden_cot * up_value * sigmoid_gate * (1.0 + gate_value * (1.0 - sigmoid_gate))
        ).astype(jnp.bfloat16)
        up_cot = (hidden_cot * active).astype(jnp.bfloat16)
        down_grad = jnp.einsum(
            "eth,etd->ehd", hidden, slot_cot, preferred_element_type=jnp.float32
        )
        joint_cot = jnp.concatenate([gate_cot, up_cot], axis=2)
        joint_grad = jnp.einsum(
            "td,eth->edh", chunk_tokens, joint_cot, preferred_element_type=jnp.float32
        )
        gate_grad = joint_grad[..., :hidden_width]
        up_grad = joint_grad[..., hidden_width:]
        input_cot = as_bf16(
            jnp.einsum("eth,edh->etd", joint_cot, joint_matrix, preferred_element_type=jnp.float32)
        )
        input_part = jnp.sum(input_cot, axis=0)
        return mixed_part, input_part, gate_grad, up_grad, down_grad

    group_count = group_tokens.shape[0]
    chunk = min(group_count, CHUNK_ROWS)
    chunks = group_count // chunk
    if chunks == 1:
        mixed_part, input_part, gate_grad, up_grad, down_grad = chunk_pass(
            group_tokens, group_cot, local_weight
        )
    else:

        def step(carry, packed):
            parts = chunk_pass(*packed)
            grads = tuple(acc + part for acc, part in zip(carry, parts[2:]))
            return grads, parts[:2]

        zeros = (
            jnp.zeros(gate_matrix.shape, jnp.float32),
            jnp.zeros(up_matrix.shape, jnp.float32),
            jnp.zeros(down_matrix.shape, jnp.float32),
        )
        packed = (
            group_tokens.reshape(chunks, chunk, -1),
            group_cot.reshape(chunks, chunk, -1),
            jnp.transpose(local_weight.reshape(local_experts, chunks, chunk, 1), (1, 0, 2, 3)),
        )
        (gate_grad, up_grad, down_grad), (mixed_parts, input_parts) = lax.scan(
            step, zeros, packed
        )
        mixed_part = mixed_parts.reshape(group_count, -1)
        input_part = input_parts.reshape(group_count, -1)
    gate_grad = gate_grad.astype(jnp.bfloat16)
    up_grad = up_grad.astype(jnp.bfloat16)
    mixed = reduce_scatter(mixed_part).astype(jnp.bfloat16)
    input_grad = reduce_scatter(input_part).astype(jnp.bfloat16)

    peers = [shifted(down_weight, "rep", 1 << bit_index) for bit_index in range(ROUNDS)]
    peer_down = peers[0]
    for bit_index in range(1, ROUNDS):
        peer_down = jnp.where(round_k[0] == bit_index, peers[bit_index], peer_down)
    bias_one = 1.0 - beta_one**step_count
    bias_two = 1.0 - beta_two**step_count
    first = beta_one * moment1[0] + (1.0 - beta_one) * down_grad
    second = beta_two * moment2[0] + (1.0 - beta_two) * down_grad * down_grad
    own_down = down_matrix.astype(jnp.float32)
    averaged = (own_down + peer_down[0].astype(jnp.float32)) * 0.5
    update = first / bias_one / (jnp.sqrt(second / bias_two) + adam_eps)
    new_down = (averaged - learn_rate * (update + decay_rate * own_down)).astype(jnp.bfloat16)
    return (
        mixed,
        input_grad,
        gate_grad[None],
        up_grad[None],
        new_down[None],
        first[None],
        second[None],
    )


def solution(mesh):
    return jax.shard_map(
        per_device,
        mesh=mesh,
        in_specs=(
            P(("rep", "exp"), None),
            P(("rep", "exp"), None),
            P(("rep", "exp"), None),
            P(("rep", "exp"), None),
            P("rep", "exp", None, None),
            P("rep", "exp", None, None),
            P("rep", "exp", None, None),
            P("rep", "exp", None, None),
            P("rep", "exp", None, None),
            P("exp"),
        ),
        out_specs=(
            P(("rep", "exp"), None),
            P(("rep", "exp"), None),
            P("rep", "exp", None, None),
            P("rep", "exp", None, None),
            P("rep", "exp", None, None),
            P("rep", "exp", None, None),
            P("rep", "exp", None, None),
        ),
        check_vma=False,
    )
```
